32 devices in a mesh: grp: 4 (over y, core), shard: 8 (over z, x).
Axes of the slice: x: 2, y: 2, z: 4, core: 2. Of those that a mesh axis runs over, the one named last changes fastest.
Arguments:
- query_rows: bfloat16 [16, 6144], P('grp'), may hold values from -10 to 10
- key_cache: bfloat16 [16, 2048, 1024], P('grp', 'shard'), may hold values from -10 to 10
- value_cache: bfloat16 [16, 2048, 1024], P('grp', 'shard'), may hold values from -6 to 6
- lengths: int32 [16], P('grp'), may hold values from 2 to 2048
- attn_gain: float32 [6144], replicated, may hold values from 0.5 to 1.5
- router: bfloat16 [6144, 4], replicated, may hold values from -0.078125 to 0.078125
- expert_ids: int32 [16, 2], replicated, may hold values from 0 to 3, all different within a row; in each aligned block of 4 rows (0 to 3, 4 to 7, ...) at most 2 rows name the same one
- w_gate: bfloat16 [4, 6144, 8192], P('grp', None, 'shard'), may hold values from -0.078125 to 0.078125
- w_up: bfloat16 [4, 6144, 8192], P('grp', None, 'shard'), may hold values from -0.078125 to 0.078125
- w_down: bfloat16 [4, 8192, 6144], P('grp', 'shard'), may hold values from -0.0625 to 0.0625
Outputs:
- normed: bfloat16 [16, 6144], P('grp')
- expert_out: bfloat16 [16, 6144], P('grp', 'shard')
The draws below stay inside these ranges and needn't reach their ends.
Inputs may be any that keep to these rules, and one draw needn't show every extreme that they name: `expert_ids`: the two ids of a row differ. Among the 4 rows of one index of grp (aligned blocks), no expert is named by more than 2 rows, a bound that some block reaches.
All inputs are finite; a program needn't handle non-finite values.
Results may differ from the reference program's by a relative error of at most 0.0095.
Values may be sent and summed in bfloat16 or wider, within the bound.
No kernel may reach another device: no remote copies, remote signals or barrier semaphores. Data moves between devices by JAX's collectives and lax.ppermute only.
A program may use at most 128 MiB of HBM per device.

```python
import math
import jax
import jax.numpy as jnp
import numpy as np
from jax import lax

D = 6144
HEADS = 48
KV_HEADS = 8
HEAD_DIM = 128
FF = 8192
ROWS_GRP = 4
CTX_DEV = 256
EXPERTS = 4
ROWS = 16
CTX = 2048
CAP = 2


def draw_query_rows(key, part):
    own_key = jax.random.fold_in(key, 23)
    shape = (ROWS, D)
    return jnp.clip(jax.random.normal(own_key, shape, jnp.float32), -6.0, 6.0).astype(jnp.bfloat16)


def draw_key_cache(key, part):
    own_key = jax.random.fold_in(key, 29)
    width = KV_HEADS * HEAD_DIM
    shape = (ROWS, CTX, width)
    return jnp.clip(jax.random.normal(own_key, shape, jnp.float32), -6.0, 6.0).astype(jnp.bfloat16)


def draw_lengths(key, part):
    own_key = jax.random.fold_in(key, 37)
    key_raw, key_shift, key_long = jax.random.split(own_key, 3)
    raw_length = jax.random.randint(key_raw, (ROWS,), 2, CTX + 1)
    shift_count = jax.random.randint(key_shift, (ROWS,), 0, 3)
    shorter = jnp.maximum(jnp.right_shift(raw_length, shift_count), 2)
    longest = jax.random.randint(key_long, (), 0, ROWS)
    return jnp.where(jnp.arange(ROWS) == longest, CTX, shorter).astype(jnp.int32)


def levels(stream_key, shape, pieces, low, largest):
    factor_of, own = 1.0, jax.random.fold_in(stream_key, 6)
    for dim, parts in pieces:
        heights = jnp.exp(jax.random.uniform(jax.random.fold_in(own, dim), (parts,), jnp.float32, low / len(pieces), largest / len(pieces)))
        factor_of = factor_of * jnp.repeat(heights, shape[dim] // parts).reshape([-1 if axis == dim else 1 for axis in range(len(shape))])
    return factor_of


def assign_block(key, own, number, rows, count, top, limit, slope):
    ranking = jax.random.permutation(key, count)
    packed, ordinary = shares(count, rows * top, limit, slope, True), shares(count, rows * top, limit, slope, False)
    places = jnp.arange(count)

    def named(tallies, offset_by):
        used = int((tallies > 0).sum())
        fixed = max(1, used // 4)
        moved = fixed + (places - fixed + offset_by * (used - fixed)) % max(1, count - fixed)
        return jnp.zeros((count,), jnp.int32).at[ranking[jnp.where(places < fixed, places, moved)]].set(jnp.asarray(tallies, jnp.int32))

    tallies = jnp.where(number % 4 == 0, named(packed, number // 4), named(ordinary, number - number // 4 - 1))
    mixed = jax.random.permutation(jax.random.fold_in(own, 3), count)
    donor, taker = mixed[0:count // 2 * 2:2], mixed[1:count // 2 * 2:2]
    slack = jnp.minimum(tallies[donor] - 1, limit - tallies[taker]) // 2
    slack = jnp.where((donor == ranking[0]) | (taker == ranking[0]) | (tallies[taker] == 0), 0, jnp.maximum(slack, 0))
    moved = jax.random.randint(jax.random.fold_in(own, 4), (count // 2,), 0, 1 << 20) % (slack + 1)
    tallies = tallies.at[donor].add(-moved).at[taker].add(moved)
    members = jnp.searchsorted(jnp.cumsum(tallies), jnp.arange(rows * top), side="right").astype(jnp.int32)
    grid = members.reshape(top, rows).T
    grid = grid[jax.random.permutation(jax.random.fold_in(own, 1), rows)]
    offset_by = jax.random.randint(jax.random.fold_in(own, 2), (rows, 1), 0, top)
    return jnp.take_along_axis(grid, (jnp.arange(top)[None, :] + offset_by) % top, axis=1)


def shares(amount, total, bound, lean, full):
    portions = [(1 << 20) // math.isqrt(standing ** lean) + 1 for standing in range(1, amount + 1)]
    largest = bound if full else min(bound, max(-(-total // amount), total * portions[0] // sum(portions)))
    least = 1 if total - largest >= amount - 1 else 0
    given, rest = [largest] + [least] * (amount - 1), total - largest - least * (amount - 1)
    while rest > 0:
        free = [i for i in range(1, amount) if given[i] < largest] or [i for i in range(1, amount) if given[i] < bound]
        mass, budget = sum([portions[i] for i in free]), rest
        for i in free:
            addition = min(bound - given[i], max(1, budget * portions[i] // mass), rest)
            given[i] = given[i] + addition
            rest = rest - addition
    return np.array(given)


def bell_draw(rng, shape, spread, limit, shards=(), kind=jnp.bfloat16):
    result = spread * jax.random.normal(rng, shape, jnp.float32)
    if shards:
        result = result * levels(rng, shape, shards, -0.22, 0.18)
    return jnp.clip(result, -limit, limit).astype(kind)


def setup_inputs(seed: int = 0) -> dict:
    keys = jax.random.split(jax.random.key(seed), 11)
    query_rows = draw_query_rows(jax.random.fold_in(keys[10], 71), 0)
    key_cache = draw_key_cache(jax.random.fold_in(keys[10], 71), 0)
    value_cache = bell_draw(keys[2], (ROWS, CTX, KV_HEADS * HEAD_DIM), 1.0, 6.0, ((0, 4), (1, 8)))
    lengths = draw_lengths(jax.random.fold_in(keys[10], 71), 0)
    attn_gain = jnp.clip(1.0 + 0.1 * jax.random.normal(keys[4], (D,), jnp.float32), 0.5, 1.5)
    router = bell_draw(keys[5], (D, EXPERTS), D ** -0.5, 0.078125)
    expert_ids_keys = jax.random.split(jax.random.fold_in(keys[6], 1), ROWS // ROWS_GRP)
    expert_ids_turns = jax.random.permutation(jax.random.fold_in(keys[6], 3), ROWS // ROWS_GRP)
    expert_ids = jax.vmap(lambda own, number: assign_block(jax.random.fold_in(keys[6], 2), own, number, ROWS_GRP, EXPERTS, 2, CAP, 2))(expert_ids_keys, expert_ids_turns).reshape((ROWS, 2))
    w_gate = bell_draw(keys[7], (EXPERTS, D, FF), D ** -0.5, 0.078125, ((0, 4), (2, 8)))
    w_up = bell_draw(keys[8], (EXPERTS, D, FF), D ** -0.5, 0.078125, ((0, 4), (2, 8)))
    w_down = bell_draw(keys[9], (EXPERTS, FF, D), FF ** -0.5, 0.0625, ((0, 4), (1, 8)))
    return {"query_rows": query_rows, "key_cache": key_cache, "value_cache": value_cache, "lengths": lengths, "attn_gain": attn_gain, "router": router, "expert_ids": expert_ids, "w_gate": w_gate, "w_up": w_up, "w_down": w_down}


NEG_FILL = -1e+30

def row_attention(inputs):
    query_row, key_row, value_row, length = inputs
    kv_share = HEADS // KV_HEADS
    blocks = CTX // CTX_DEV
    query_heads = query_row.astype(jnp.float32).reshape(KV_HEADS, kv_share, HEAD_DIM)
    key_heads = key_row.astype(jnp.float32).reshape(CTX, KV_HEADS, HEAD_DIM)
    value_heads = value_row.astype(jnp.float32).reshape(blocks, CTX_DEV, KV_HEADS, HEAD_DIM)
    scores = jnp.einsum('gjd,tgd->gjt', query_heads, key_heads) / math.sqrt(HEAD_DIM)
    live_mask = jnp.arange(CTX) < length
    scores = jnp.where(live_mask, scores, NEG_FILL)
    score_blocks = scores.reshape(KV_HEADS, kv_share, blocks, CTX_DEV)
    live_blocks = live_mask.reshape(blocks, CTX_DEV)
    block_max = lax.optimization_barrier(jnp.max(score_blocks, axis=-1))
    block_probs = jnp.where(live_blocks, jnp.exp(score_blocks - block_max[..., None]), 0.0).astype(jnp.bfloat16)
    probs_wide = block_probs.astype(jnp.float32)
    block_sum = lax.optimization_barrier(jnp.sum(probs_wide, axis=-1))
    block_mix = jnp.einsum('gjbt,btgd->gjbd', probs_wide, value_heads)
    top_max = lax.optimization_barrier(jnp.max(block_max, axis=-1))
    factor = jnp.exp(block_max - top_max[..., None])
    whole_sum = lax.optimization_barrier(jnp.sum(block_sum * factor, axis=-1))
    whole_mix = lax.optimization_barrier(jnp.sum(block_mix * factor[..., None], axis=-2))
    return (whole_mix / whole_sum[..., None]).reshape(D)

def reference(query_rows, key_cache, value_cache, lengths, attn_gain, router, expert_ids, w_gate, w_up, w_down):
    attended = lax.map(row_attention, (query_rows, key_cache, value_cache, lengths))
    mean_square = lax.optimization_barrier(jnp.mean(attended * attended, axis=-1, keepdims=True))
    normed = (attended * lax.rsqrt(mean_square + 1e-05) * attn_gain).astype(jnp.bfloat16)
    logits = jnp.dot(normed, router, preferred_element_type=jnp.float32)
    expert_hit = expert_ids[:, :, None] == jnp.arange(EXPERTS, dtype=jnp.int32)[None, None, :]
    chosen = lax.optimization_barrier(jnp.sum(jnp.where(expert_hit, logits[:, None, :], 0.0), axis=-1))
    first_weight = jax.nn.sigmoid(chosen[:, 0] - chosen[:, 1])
    route_weight = jnp.stack([first_weight, 1.0 - first_weight], axis=1)

    def one_expert(running_sum, expert_index):
        gate_proj = jnp.dot(normed, w_gate[expert_index], preferred_element_type=jnp.float32)
        up_proj = jnp.dot(normed, w_up[expert_index], preferred_element_type=jnp.float32)
        hidden = (jax.nn.silu(gate_proj) * up_proj).astype(jnp.bfloat16)
        expert_y = jnp.dot(hidden, w_down[expert_index], preferred_element_type=jnp.float32)
        coefficient = lax.optimization_barrier(jnp.sum(jnp.where(expert_ids == expert_index, route_weight, 0.0), axis=-1))
        return (running_sum + coefficient[:, None] * expert_y, None)
    starting = jnp.zeros((ROWS, D), jnp.float32)
    combined, _ = lax.scan(one_expert, starting, jnp.arange(EXPERTS, dtype=jnp.int32))
    return (normed, combined.astype(jnp.bfloat16))
```

```python
import math

import jax
import jax.numpy as jnp
from jax import lax
from jax.sharding import PartitionSpec as P

HEADS = 48
KV_HEADS = 8
HEAD_DIM = 128
BLOCK = 256


NEG_FILL = -1e30


def shards(
    query_rows, key_cache, value_cache, lengths, attn_gain, router, expert_ids, w_gate, w_up, w_down
):
    rows_here = query_rows.shape[0]
    span = key_cache.shape[1]
    kv_share = HEADS // KV_HEADS
    n_grp = lax.axis_size("grp")
    n_shard = lax.axis_size("shard")
    grp_id = lax.axis_index("grp")
    shard_id = lax.axis_index("shard")
    n_blocks = span // BLOCK

    query_heads = query_rows.reshape(rows_here, KV_HEADS, kv_share, HEAD_DIM)
    key_heads = key_cache.reshape(rows_here, span, KV_HEADS, HEAD_DIM)
    value_heads = value_cache.reshape(rows_here, n_blocks, BLOCK, KV_HEADS, HEAD_DIM)
    scores = jnp.einsum(
        "rgjd,rtgd->rgjt", query_heads, key_heads, preferred_element_type=jnp.float32
    ) / math.sqrt(HEAD_DIM)
    position = shard_id * span + jnp.arange(span, dtype=jnp.int32)
    live_mask = (position[None, :] < lengths[:, None])[:, None, None, :]
    scores = jnp.where(live_mask, scores, NEG_FILL)
    scores = scores.reshape(rows_here, KV_HEADS, kv_share, n_blocks, BLOCK)
    live_blocks = live_mask.reshape(rows_here, 1, 1, n_blocks, BLOCK)
    block_max = jnp.max(scores, axis=-1)
    block_probs = jnp.where(live_blocks, jnp.exp(scores - block_max[..., None]), 0.0).astype(
        jnp.bfloat16
    )
    block_sum = jnp.sum(block_probs.astype(jnp.float32), axis=-1)
    block_mix = jnp.einsum(
        "rgjbt,rbtgd->rgjbd", block_probs, value_heads, preferred_element_type=jnp.float32
    )
    dev_max = jnp.max(block_max, axis=-1)
    dev_factor = jnp.exp(block_max - dev_max[..., None])
    dev_sum = jnp.sum(block_sum * dev_factor, axis=-1).reshape(rows_here, HEADS)
    dev_mix = jnp.sum(block_mix * dev_factor[..., None], axis=-2).reshape(rows_here, HEADS, HEAD_DIM)
    dev_max = dev_max.reshape(rows_here, HEADS)

    per_chunk = HEADS // n_shard
    mix_out = dev_mix.reshape(rows_here, n_shard, per_chunk, HEAD_DIM)
    side = jnp.concatenate(
        [dev_max.reshape(rows_here, n_shard, per_chunk), dev_sum.reshape(rows_here, n_shard, per_chunk)],
        axis=-1,
    )
    side = jnp.pad(side, ((0, 0), (0, 0), (0, HEAD_DIM - 2 * per_chunk)))
    packed = jnp.concatenate([mix_out, side[:, :, None, :]], axis=2)
    packed = jnp.transpose(packed, (1, 0, 2, 3))
    stats = lax.all_to_all(packed, "shard", 0, 0, tiled=True)
    got_mix = stats[:, :, :per_chunk, :]
    got_max = stats[:, :, per_chunk, :per_chunk]
    got_sum = stats[:, :, per_chunk, per_chunk : 2 * per_chunk]
    top = jnp.max(got_max, axis=0)
    factor = jnp.exp(got_max - top[None])
    whole_sum = jnp.sum(got_sum * factor, axis=0)
    whole_mix = jnp.sum(got_mix * factor[..., None], axis=0)
    chunk = (whole_mix / whole_sum[..., None]).reshape(rows_here, per_chunk * HEAD_DIM)

    n_dev = n_grp * n_shard
    spread = jnp.broadcast_to(chunk[None], (n_dev,) + chunk.shape)
    gathered = lax.all_to_all(spread, ("grp", "shard"), 0, 0, tiled=True)
    gathered = gathered.reshape(n_grp, n_shard, rows_here, per_chunk * HEAD_DIM)
    attended = jnp.transpose(gathered, (0, 2, 1, 3)).reshape(n_grp * rows_here, -1)

    mean_square = jnp.mean(attended * attended, axis=-1, keepdims=True)
    normed_all = (attended * lax.rsqrt(mean_square + 1e-05) * attn_gain).astype(jnp.bfloat16)
    normed = lax.dynamic_slice_in_dim(normed_all, grp_id * rows_here, rows_here, 0)

    logits = jnp.dot(normed_all, router, preferred_element_type=jnp.float32)
    experts = router.shape[1]
    expert_range = jnp.arange(experts, dtype=jnp.int32)
    expert_hit = expert_ids[:, :, None] == expert_range[None, None, :]
    chosen = jnp.sum(jnp.where(expert_hit, logits[:, None, :], 0.0), axis=-1)
    first_weight = jax.nn.sigmoid(chosen[:, 0] - chosen[:, 1])
    route_weight = jnp.stack([first_weight, 1.0 - first_weight], axis=1)

    local_experts = w_gate.shape[0]
    width = normed_all.shape[1]
    total = jnp.zeros((n_grp * rows_here, width), jnp.float32)
    for local in range(local_experts):
        expert_index = grp_id * local_experts + local
        coefficient = jnp.sum(jnp.where(expert_ids == expert_index, route_weight, 0.0), axis=-1)
        gate_proj = jnp.dot(normed_all, w_gate[local], preferred_element_type=jnp.float32)
        up_proj = jnp.dot(normed_all, w_up[local], preferred_element_type=jnp.float32)
        hidden = (jax.nn.silu(gate_proj) * up_proj).astype(jnp.bfloat16)
        expert_y = jnp.dot(hidden, w_down[local], preferred_element_type=jnp.float32)
        total = total + coefficient[:, None] * expert_y

    out_width = width // n_shard
    blocks = total.reshape(n_grp, rows_here, n_shard, out_width)
    blocks = jnp.transpose(blocks, (0, 2, 1, 3)).reshape(n_dev, rows_here, out_width)
    arrived = lax.all_to_all(blocks, ("grp", "shard"), 0, 0, tiled=True)
    result = jnp.sum(arrived, axis=0)
    return (normed, result.astype(jnp.bfloat16))


def solution(mesh):
    in_specs = (
        P("grp", None),
        P("grp", "shard", None),
        P("grp", "shard", None),
        P("grp"),
        P(),
        P(),
        P(),
        P("grp", None, "shard"),
        P("grp", None, "shard"),
        P("grp", "shard", None),
    )
    out_specs = (P("grp", None), P("grp", "shard"))
    return jax.shard_map(shards, mesh=mesh, in_specs=in_specs, out_specs=out_specs, check_vma=False)
```

```python
import math

import jax
import jax.numpy as jnp
from jax import lax
from jax.sharding import PartitionSpec as P

HEADS = 48
KV_HEADS = 8
HEAD_DIM = 128
BLOCK = 256


NEG_FILL = -1e30


def shards(
    query_rows, key_cache, value_cache, lengths, attn_gain, router, expert_ids, w_gate, w_up, w_down
):
    rows_here = query_rows.shape[0]
    span = key_cache.shape[1]
    kv_share = HEADS // KV_HEADS
    n_grp = lax.axis_size("grp")
    n_shard = lax.axis_size("shard")
    grp_id = lax.axis_index("grp")
    shard_id = lax.axis_index("shard")
    n_blocks = span // BLOCK

    query_heads = query_rows.reshape(rows_here, KV_HEADS, kv_share, HEAD_DIM)
    key_heads = key_cache.reshape(rows_here, span, KV_HEADS, HEAD_DIM)
    value_heads = value_cache.reshape(rows_here, n_blocks, BLOCK, KV_HEADS, HEAD_DIM)
    scores = jnp.einsum(
        "rgjd,rtgd->rgjt", query_heads, key_heads, preferred_element_type=jnp.float32
    ) / math.sqrt(HEAD_DIM)
    position = shard_id * span + jnp.arange(span, dtype=jnp.int32)
    live_mask = (position[None, :] < lengths[:, None])[:, None, None, :]
    scores = jnp.where(live_mask, scores, NEG_FILL)
    scores = scores.reshape(rows_here, KV_HEADS, kv_share, n_blocks, BLOCK)
    live_blocks = live_mask.reshape(rows_here, 1, 1, n_blocks, BLOCK)
    block_max = jnp.max(scores, axis=-1)
    block_probs = jnp.where(live_blocks, jnp.exp(scores - block_max[..., None]), 0.0).astype(
        jnp.bfloat16
    )
    block_sum = jnp.sum(block_probs.astype(jnp.float32), axis=-1)
    block_mix = jnp.einsum(
        "rgjbt,rbtgd->rgjbd", block_probs, value_heads, preferred_element_type=jnp.float32
    )
    dev_max = jnp.max(block_max, axis=-1)
    dev_factor = jnp.exp(block_max - dev_max[..., None])
    dev_sum = jnp.sum(block_sum * dev_factor, axis=-1).reshape(rows_here, HEADS)
    dev_mix = jnp.sum(block_mix * dev_factor[..., None], axis=-2).reshape(rows_here, HEADS, HEAD_DIM)
    dev_max = dev_max.reshape(rows_here, HEADS)

    per_chunk = HEADS // n_shard
    mix_out = dev_mix.reshape(rows_here, n_shard, per_chunk, HEAD_DIM)
    side = jnp.concatenate(
        [dev_max.reshape(rows_here, n_shard, per_chunk), dev_sum.reshape(rows_here, n_shard, per_chunk)],
        axis=-1,
    )
    side = jnp.pad(side, ((0, 0), (0, 0), (0, HEAD_DIM - 2 * per_chunk)))
    packed = jnp.concatenate([mix_out, side[:, :, None, :]], axis=2)
    packed = jnp.transpose(packed, (1, 0, 2, 3))
    stats = lax.all_to_all(packed, "shard", 0, 0, tiled=True)
    got_mix = stats[:, :, :per_chunk, :]
    got_max = stats[:, :, per_chunk, :per_chunk]
    got_sum = stats[:, :, per_chunk, per_chunk : 2 * per_chunk]
    top = jnp.max(got_max, axis=0)
    factor = jnp.exp(got_max - top[None])
    whole_sum = jnp.sum(got_sum * factor, axis=0)
    whole_mix = jnp.sum(got_mix * factor[..., None], axis=0)
    chunk = (whole_mix / whole_sum[..., None]).reshape(rows_here, per_chunk * HEAD_DIM)

    n_dev = n_grp * n_shard
    spread = jnp.broadcast_to(chunk.astype(jnp.bfloat16)[None], (n_dev,) + chunk.shape)
    gathered = lax.all_to_all(spread, ("grp", "shard"), 0, 0, tiled=True).astype(jnp.float32)
    gathered = gathered.reshape(n_grp, n_shard, rows_here, per_chunk * HEAD_DIM)
    attended = jnp.transpose(gathered, (0, 2, 1, 3)).reshape(n_grp * rows_here, -1)

    mean_square = jnp.mean(attended * attended, axis=-1, keepdims=True)
    normed_all = (attended * lax.rsqrt(mean_square + 1e-05) * attn_gain).astype(jnp.bfloat16)
    normed = lax.dynamic_slice_in_dim(normed_all, grp_id * rows_here, rows_here, 0)

    logits = jnp.dot(normed_all, router, preferred_element_type=jnp.float32)
    experts = router.shape[1]
    expert_range = jnp.arange(experts, dtype=jnp.int32)
    expert_hit = expert_ids[:, :, None] == expert_range[None, None, :]
    chosen = jnp.sum(jnp.where(expert_hit, logits[:, None, :], 0.0), axis=-1)
    first_weight = jax.nn.sigmoid(chosen[:, 0] - chosen[:, 1])
    route_weight = jnp.stack([first_weight, 1.0 - first_weight], axis=1)

    local_experts = w_gate.shape[0]
    width = normed_all.shape[1]
    total = jnp.zeros((n_grp * rows_here, width), jnp.float32)
    for local in range(local_experts):
        expert_index = grp_id * local_experts + local
        coefficient = jnp.sum(jnp.where(expert_ids == expert_index, route_weight, 0.0), axis=-1)
        gate_proj = jnp.dot(normed_all, w_gate[local], preferred_element_type=jnp.float32)
        up_proj = jnp.dot(normed_all, w_up[local], preferred_element_type=jnp.float32)
        hidden = (jax.nn.silu(gate_proj) * up_proj).astype(jnp.bfloat16)
        expert_y = jnp.dot(hidden, w_down[local], preferred_element_type=jnp.float32)
        total = total + coefficient[:, None] * expert_y

    out_width = width // n_shard
    blocks = total.reshape(n_grp, rows_here, n_shard, out_width)
    blocks = jnp.transpose(blocks, (0, 2, 1, 3)).reshape(n_dev, rows_here, out_width)
    arrived = lax.all_to_all(blocks, ("grp", "shard"), 0, 0, tiled=True)
    result = jnp.sum(arrived, axis=0)
    return (normed, result.astype(jnp.bfloat16))


def solution(mesh):
    in_specs = (
        P("grp", None),
        P("grp", "shard", None),
        P("grp", "shard", None),
        P("grp"),
        P(),
        P(),
        P(),
        P("grp", None, "shard"),
        P("grp", None, "shard"),
        P("grp", "shard", None),
    )
    out_specs = (P("grp", None), P("grp", "shard"))
    return jax.shard_map(shards, mesh=mesh, in_specs=in_specs, out_specs=out_specs, check_vma=False)
```

```python
import math

import jax
import jax.numpy as jnp
from jax import lax
from jax.sharding import PartitionSpec as P

HEADS = 48
KV_HEADS = 8
HEAD_DIM = 128
BLOCK = 256


NEG_FILL = -1e30
CAP = 2


def slots_of(expert_ids, expert_index, rows_here, n_groups):
    ids = expert_ids.reshape(n_groups, rows_here, expert_ids.shape[1])
    hit = jnp.any(ids == expert_index, axis=-1)
    rank = jnp.cumsum(hit.astype(jnp.int32), axis=1) - 1
    local = jnp.arange(rows_here, dtype=jnp.int32)
    rows, live = [], []
    for slot in range(CAP):
        match = hit & (rank == slot)
        rows.append(jnp.sum(jnp.where(match, local[None, :], 0), axis=1))
        live.append(jnp.any(match, axis=1))
    return jnp.stack(rows, axis=1), jnp.stack(live, axis=1)


def shards(
    query_rows, key_cache, value_cache, lengths, attn_gain, router, expert_ids, w_gate, w_up, w_down
):
    rows_here = query_rows.shape[0]
    span = key_cache.shape[1]
    kv_share = HEADS // KV_HEADS
    n_grp = lax.axis_size("grp")
    n_shard = lax.axis_size("shard")
    grp_id = lax.axis_index("grp")
    shard_id = lax.axis_index("shard")
    n_blocks = span // BLOCK

    query_heads = query_rows.reshape(rows_here, KV_HEADS, kv_share, HEAD_DIM)
    key_heads = key_cache.reshape(rows_here, span, KV_HEADS, HEAD_DIM)
    value_heads = value_cache.reshape(rows_here, n_blocks, BLOCK, KV_HEADS, HEAD_DIM)
    scores = jnp.einsum(
        "rgjd,rtgd->rgjt", query_heads, key_heads, preferred_element_type=jnp.float32
    ) / math.sqrt(HEAD_DIM)
    position = shard_id * span + jnp.arange(span, dtype=jnp.int32)
    live_mask = (position[None, :] < lengths[:, None])[:, None, None, :]
    scores = jnp.where(live_mask, scores, NEG_FILL)
    scores = scores.reshape(rows_here, KV_HEADS, kv_share, n_blocks, BLOCK)
    live_blocks = live_mask.reshape(rows_here, 1, 1, n_blocks, BLOCK)
    block_max = jnp.max(scores, axis=-1)
    block_probs = jnp.where(live_blocks, jnp.exp(scores - block_max[..., None]), 0.0).astype(
        jnp.bfloat16
    )
    block_sum = jnp.sum(block_probs.astype(jnp.float32), axis=-1)
    block_mix = jnp.einsum(
        "rgjbt,rbtgd->rgjbd", block_probs, value_heads, preferred_element_type=jnp.float32
    )
    dev_max = jnp.max(block_max, axis=-1)
    dev_factor = jnp.exp(block_max - dev_max[..., None])
    dev_sum = jnp.sum(block_sum * dev_factor, axis=-1).reshape(rows_here, HEADS)
    dev_mix = jnp.sum(block_mix * dev_factor[..., None], axis=-2).reshape(rows_here, HEADS, HEAD_DIM)
    dev_max = dev_max.reshape(rows_here, HEADS)

    per_chunk = HEADS // n_shard
    mix_out = dev_mix.reshape(rows_here, n_shard, per_chunk, HEAD_DIM)
    side = jnp.concatenate(
        [dev_max.reshape(rows_here, n_shard, per_chunk), dev_sum.reshape(rows_here, n_shard, per_chunk)],
        axis=-1,
    )
    side = jnp.pad(side, ((0, 0), (0, 0), (0, HEAD_DIM - 2 * per_chunk)))
    packed = jnp.concatenate([mix_out, side[:, :, None, :]], axis=2)
    packed = jnp.transpose(packed, (1, 0, 2, 3))
    stats = lax.all_to_all(packed, "shard", 0, 0, tiled=True)
    got_mix = stats[:, :, :per_chunk, :]
    got_max = stats[:, :, per_chunk, :per_chunk]
    got_sum = stats[:, :, per_chunk, per_chunk : 2 * per_chunk]
    top = jnp.max(got_max, axis=0)
    factor = jnp.exp(got_max - top[None])
    whole_sum = jnp.sum(got_sum * factor, axis=0)
    whole_mix = jnp.sum(got_mix * factor[..., None], axis=0)
    chunk = (whole_mix / whole_sum[..., None]).reshape(rows_here, per_chunk * HEAD_DIM)

    n_dev = n_grp * n_shard
    spread = jnp.broadcast_to(chunk.astype(jnp.bfloat16)[None], (n_dev,) + chunk.shape)
    gathered = lax.all_to_all(spread, ("grp", "shard"), 0, 0, tiled=True).astype(jnp.float32)
    gathered = gathered.reshape(n_grp, n_shard, rows_here, per_chunk * HEAD_DIM)
    attended = jnp.transpose(gathered, (0, 2, 1, 3)).reshape(n_grp * rows_here, -1)

    mean_square = jnp.mean(attended * attended, axis=-1, keepdims=True)
    normed_all = (attended * lax.rsqrt(mean_square + 1e-05) * attn_gain).astype(jnp.bfloat16)
    normed = lax.dynamic_slice_in_dim(normed_all, grp_id * rows_here, rows_here, 0)

    logits = jnp.dot(normed_all, router, preferred_element_type=jnp.float32)
    experts = router.shape[1]
    expert_range = jnp.arange(experts, dtype=jnp.int32)
    expert_hit = expert_ids[:, :, None] == expert_range[None, None, :]
    chosen = jnp.sum(jnp.where(expert_hit, logits[:, None, :], 0.0), axis=-1)
    first_weight = jax.nn.sigmoid(chosen[:, 0] - chosen[:, 1])
    route_weight = jnp.stack([first_weight, 1.0 - first_weight], axis=1)

    local_experts = w_gate.shape[0]
    assert local_experts == 1
    width = normed_all.shape[1]
    total = jnp.zeros((n_grp * rows_here, width), jnp.float32)
    for local in range(local_experts):
        expert_index = grp_id * local_experts + local
        coefficient = jnp.sum(jnp.where(expert_ids == expert_index, route_weight, 0.0), axis=-1)
        gate_proj = jnp.dot(normed_all, w_gate[local], preferred_element_type=jnp.float32)
        up_proj = jnp.dot(normed_all, w_up[local], preferred_element_type=jnp.float32)
        hidden = (jax.nn.silu(gate_proj) * up_proj).astype(jnp.bfloat16)
        expert_y = jnp.dot(hidden, w_down[local], preferred_element_type=jnp.float32)
        total = total + coefficient[:, None] * expert_y

    out_width = width // n_shard
    picked_rows, picked_live = slots_of(expert_ids, grp_id * local_experts, rows_here, n_grp)
    grouped = total.reshape(n_grp, rows_here, width)
    picked = jnp.take_along_axis(grouped, picked_rows[:, :, None], axis=1)
    picked = jnp.where(picked_live[:, :, None], picked, 0.0)
    blocks = picked.reshape(n_grp, CAP, n_shard, out_width)
    blocks = jnp.transpose(blocks, (0, 2, 1, 3)).reshape(n_dev, CAP, out_width)
    arrived = lax.all_to_all(blocks, ("grp", "shard"), 0, 0, tiled=True)
    per_expert = jnp.sum(arrived.reshape(n_grp, n_shard, CAP, out_width), axis=1)
    own_ids = lax.dynamic_slice_in_dim(expert_ids, grp_id * rows_here, rows_here, 0)
    result = jnp.zeros((rows_here, out_width), jnp.float32)
    for source in range(n_grp):
        home_rows, home_live = slots_of(own_ids, source * local_experts, rows_here, 1)
        for slot in range(CAP):
            hit = (jnp.arange(rows_here) == home_rows[0, slot]) & home_live[0, slot]
            result = result + jnp.where(hit[:, None], per_expert[source, slot][None, :], 0.0)
    return (normed, result.astype(jnp.bfloat16))


def solution(mesh):
    in_specs = (
        P("grp", None),
        P("grp", "shard", None),
        P("grp", "shard", None),
        P("grp"),
        P(),
        P(),
        P(),
        P("grp", None, "shard"),
        P("grp", None, "shard"),
        P("grp", "shard", None),
    )
    out_specs = (P("grp", None), P("grp", "shard"))
    return jax.shard_map(shards, mesh=mesh, in_specs=in_specs, out_specs=out_specs, check_vma=False)
```

```python
import math

import jax
import jax.numpy as jnp
from jax import lax
from jax.sharding import PartitionSpec as P

HEADS = 48
KV_HEADS = 8
HEAD_DIM = 128
BLOCK = 256


NEG_FILL = -1e30
CAP = 2


def slot_match(expert_ids, experts, rows_here, n_groups):
    ids = expert_ids.reshape(n_groups, rows_here, expert_ids.shape[1])
    hit = jnp.any(ids[None, :, :, :] == experts[:, None, None, None], axis=-1)
    rank = jnp.cumsum(hit.astype(jnp.int32), axis=-1) - 1
    slot = jnp.arange(CAP, dtype=jnp.int32)
    return hit[:, :, None, :] & (rank[:, :, None, :] == slot[None, None, :, None])


def shards(
    query_rows, key_cache, value_cache, lengths, attn_gain, router, expert_ids, w_gate, w_up, w_down
):
    rows_here = query_rows.shape[0]
    span = key_cache.shape[1]
    kv_share = HEADS // KV_HEADS
    n_grp = lax.axis_size("grp")
    n_shard = lax.axis_size("shard")
    grp_id = lax.axis_index("grp")
    shard_id = lax.axis_index("shard")
    n_blocks = span // BLOCK

    query_heads = query_rows.reshape(rows_here, KV_HEADS, kv_share, HEAD_DIM)
    key_heads = key_cache.reshape(rows_here, span, KV_HEADS, HEAD_DIM)
    value_heads = value_cache.reshape(rows_here, n_blocks, BLOCK, KV_HEADS, HEAD_DIM)
    scores = jnp.einsum(
        "rgjd,rtgd->rgjt", query_heads, key_heads, preferred_element_type=jnp.float32
    ) / math.sqrt(HEAD_DIM)
    position = shard_id * span + jnp.arange(span, dtype=jnp.int32)
    live_mask = (position[None, :] < lengths[:, None])[:, None, None, :]
    scores = jnp.where(live_mask, scores, NEG_FILL)
    scores = scores.reshape(rows_here, KV_HEADS, kv_share, n_blocks, BLOCK)
    live_blocks = live_mask.reshape(rows_here, 1, 1, n_blocks, BLOCK)
    block_max = jnp.max(scores, axis=-1)
    block_probs = jnp.where(live_blocks, jnp.exp(scores - block_max[..., None]), 0.0).astype(
        jnp.bfloat16
    )
    block_sum = jnp.sum(block_probs.astype(jnp.float32), axis=-1)
    block_mix = jnp.einsum(
        "rgjbt,rbtgd->rgjbd", block_probs, value_heads, preferred_element_type=jnp.float32
    )
    dev_max = jnp.max(block_max, axis=-1)
    dev_factor = jnp.exp(block_max - dev_max[..., None])
    dev_sum = jnp.sum(block_sum * dev_factor, axis=-1).reshape(rows_here, HEADS)
    dev_mix = jnp.sum(block_mix * dev_factor[..., None], axis=-2).reshape(rows_here, HEADS, HEAD_DIM)
    dev_max = dev_max.reshape(rows_here, HEADS)

    per_chunk = HEADS // n_shard
    mix_out = dev_mix.reshape(rows_here, n_shard, per_chunk, HEAD_DIM)
    side = jnp.concatenate(
        [dev_max.reshape(rows_here, n_shard, per_chunk), dev_sum.reshape(rows_here, n_shard, per_chunk)],
        axis=-1,
    )
    side = jnp.pad(side, ((0, 0), (0, 0), (0, HEAD_DIM - 2 * per_chunk)))
    packed = jnp.concatenate([mix_out, side[:, :, None, :]], axis=2)
    packed = jnp.transpose(packed, (1, 0, 2, 3))
    stats = lax.all_to_all(packed, "shard", 0, 0, tiled=True)
    got_mix = stats[:, :, :per_chunk, :]
    got_max = stats[:, :, per_chunk, :per_chunk]
    got_sum = stats[:, :, per_chunk, per_chunk : 2 * per_chunk]
    top = jnp.max(got_max, axis=0)
    factor = jnp.exp(got_max - top[None])
    whole_sum = jnp.sum(got_sum * factor, axis=0)
    whole_mix = jnp.sum(got_mix * factor[..., None], axis=0)
    chunk = (whole_mix / whole_sum[..., None]).reshape(rows_here, per_chunk * HEAD_DIM)

    n_dev = n_grp * n_shard
    spread = jnp.broadcast_to(chunk.astype(jnp.bfloat16)[None], (n_dev,) + chunk.shape)
    gathered = lax.all_to_all(spread, ("grp", "shard"), 0, 0, tiled=True).astype(jnp.float32)
    gathered = gathered.reshape(n_grp, n_shard, rows_here, per_chunk * HEAD_DIM)
    attended = jnp.transpose(gathered, (0, 2, 1, 3)).reshape(n_grp * rows_here, -1)

    mean_square = jnp.mean(attended * attended, axis=-1, keepdims=True)
    normed_all = (attended * lax.rsqrt(mean_square + 1e-05) * attn_gain).astype(jnp.bfloat16)
    normed = lax.dynamic_slice_in_dim(normed_all, grp_id * rows_here, rows_here, 0)

    logits = jnp.dot(normed_all, router, preferred_element_type=jnp.float32)
    experts = router.shape[1]
    expert_range = jnp.arange(experts, dtype=jnp.int32)
    expert_hit = expert_ids[:, :, None] == expert_range[None, None, :]
    chosen = jnp.sum(jnp.where(expert_hit, logits[:, None, :], 0.0), axis=-1)
    first_weight = jax.nn.sigmoid(chosen[:, 0] - chosen[:, 1])
    route_weight = jnp.stack([first_weight, 1.0 - first_weight], axis=1)

    local_experts = w_gate.shape[0]
    assert local_experts == 1
    width = normed_all.shape[1]
    total = jnp.zeros((n_grp * rows_here, width), jnp.float32)
    for local in range(local_experts):
        expert_index = grp_id * local_experts + local
        coefficient = jnp.sum(jnp.where(expert_ids == expert_index, route_weight, 0.0), axis=-1)
        gate_proj = jnp.dot(normed_all, w_gate[local], preferred_element_type=jnp.float32)
        up_proj = jnp.dot(normed_all, w_up[local], preferred_element_type=jnp.float32)
        hidden = (jax.nn.silu(gate_proj) * up_proj).astype(jnp.bfloat16)
        expert_y = jnp.dot(hidden, w_down[local], preferred_element_type=jnp.float32)
        total = total + coefficient[:, None] * expert_y

    out_width = width // n_shard
    sending = slot_match(expert_ids, (grp_id * local_experts)[None], rows_here, n_grp)[0]
    grouped = total.reshape(n_grp, 1, rows_here, width)
    picked = jnp.sum(jnp.where(sending[..., None], grouped, 0.0), axis=2)
    blocks = picked.reshape(n_grp, CAP, n_shard, out_width)
    blocks = jnp.transpose(blocks, (0, 2, 1, 3)).reshape(n_dev, CAP, out_width)
    arrived = lax.all_to_all(blocks, ("grp", "shard"), 0, 0, tiled=True)
    per_expert = jnp.sum(arrived.reshape(n_grp, n_shard, CAP, out_width), axis=1)
    own_ids = lax.dynamic_slice_in_dim(expert_ids, grp_id * rows_here, rows_here, 0)
    homes = slot_match(own_ids, jnp.arange(n_grp, dtype=jnp.int32) * local_experts, rows_here, 1)[:, 0]
    spread_back = jnp.where(homes[..., None], per_expert[:, :, None, :], 0.0)
    result = jnp.sum(spread_back, axis=(0, 1))
    return (normed, result.astype(jnp.bfloat16))


def solution(mesh):
    in_specs = (
        P("grp", None),
        P("grp", "shard", None),
        P("grp", "shard", None),
        P("grp"),
        P(),
        P(),
        P(),
        P("grp", None, "shard"),
        P("grp", None, "shard"),
        P("grp", "shard", None),
    )
    out_specs = (P("grp", None), P("grp", "shard"))
    return jax.shard_map(shards, mesh=mesh, in_specs=in_specs, out_specs=out_specs, check_vma=False)
```

```python
import math

import jax
import jax.numpy as jnp
from jax import lax
from jax.sharding import PartitionSpec as P

HEADS = 48
KV_HEADS = 8
HEAD_DIM = 128
BLOCK = 256


NEG_FILL = -1e30
CAP = 2


def slot_match(expert_ids, experts, rows_here, n_groups):
    ids = expert_ids.reshape(n_groups, rows_here, expert_ids.shape[1])
    hit = jnp.any(ids[None, :, :, :] == experts[:, None, None, None], axis=-1)
    rank = jnp.cumsum(hit.astype(jnp.int32), axis=-1) - 1
    slot = jnp.arange(CAP, dtype=jnp.int32)
    return hit[:, :, None, :] & (rank[:, :, None, :] == slot[None, None, :, None])


def shards(
    query_rows, key_cache, value_cache, lengths, attn_gain, router, expert_ids, w_gate, w_up, w_down
):
    rows_here = query_rows.shape[0]
    span = key_cache.shape[1]
    kv_share = HEADS // KV_HEADS
    n_grp = lax.axis_size("grp")
    n_shard = lax.axis_size("shard")
    grp_id = lax.axis_index("grp")
    shard_id = lax.axis_index("shard")
    n_blocks = span // BLOCK

    query_heads = query_rows.reshape(rows_here, KV_HEADS, kv_share, HEAD_DIM)
    key_heads = key_cache.reshape(rows_here, span, KV_HEADS, HEAD_DIM)
    value_heads = value_cache.reshape(rows_here, n_blocks, BLOCK, KV_HEADS, HEAD_DIM)
    scores = jnp.einsum(
        "rgjd,rtgd->rgjt", query_heads, key_heads, preferred_element_type=jnp.float32
    ) / math.sqrt(HEAD_DIM)
    position = shard_id * span + jnp.arange(span, dtype=jnp.int32)
    live_mask = (position[None, :] < lengths[:, None])[:, None, None, :]
    scores = jnp.where(live_mask, scores, NEG_FILL)
    scores = scores.reshape(rows_here, KV_HEADS, kv_share, n_blocks, BLOCK)
    live_blocks = live_mask.reshape(rows_here, 1, 1, n_blocks, BLOCK)
    block_max = jnp.max(scores, axis=-1)
    block_probs = jnp.where(live_blocks, jnp.exp(scores - block_max[..., None]), 0.0).astype(
        jnp.bfloat16
    )
    block_sum = jnp.sum(block_probs.astype(jnp.float32), axis=-1)
    block_mix = jnp.einsum(
        "rgjbt,rbtgd->rgjbd", block_probs, value_heads, preferred_element_type=jnp.float32
    )
    dev_max = jnp.max(block_max, axis=-1)
    dev_factor = jnp.exp(block_max - dev_max[..., None])
    dev_sum = jnp.sum(block_sum * dev_factor, axis=-1).reshape(rows_here, HEADS)
    dev_mix = jnp.sum(block_mix * dev_factor[..., None], axis=-2).reshape(rows_here, HEADS, HEAD_DIM)
    dev_max = dev_max.reshape(rows_here, HEADS)

    per_chunk = HEADS // n_shard
    mix_out = dev_mix.reshape(rows_here, n_shard, per_chunk, HEAD_DIM)
    side = jnp.concatenate(
        [dev_max.reshape(rows_here, n_shard, per_chunk), dev_sum.reshape(rows_here, n_shard, per_chunk)],
        axis=-1,
    )
    side = jnp.pad(side, ((0, 0), (0, 0), (0, HEAD_DIM - 2 * per_chunk)))
    packed = jnp.concatenate([mix_out, side[:, :, None, :]], axis=2)
    packed = jnp.transpose(packed, (1, 0, 2, 3))
    stats = lax.all_to_all(packed, "shard", 0, 0, tiled=True)
    got_mix = stats[:, :, :per_chunk, :]
    got_max = stats[:, :, per_chunk, :per_chunk]
    got_sum = stats[:, :, per_chunk, per_chunk : 2 * per_chunk]
    top = jnp.max(got_max, axis=0)
    factor = jnp.exp(got_max - top[None])
    whole_sum = jnp.sum(got_sum * factor, axis=0)
    whole_mix = jnp.sum(got_mix * factor[..., None], axis=0)
    chunk = (whole_mix / whole_sum[..., None]).reshape(rows_here, per_chunk * HEAD_DIM)

    n_dev = n_grp * n_shard
    spread = jnp.broadcast_to(chunk.astype(jnp.bfloat16)[None], (n_dev,) + chunk.shape)
    gathered = lax.all_to_all(spread, ("grp", "shard"), 0, 0, tiled=True).astype(jnp.float32)
    gathered = gathered.reshape(n_grp, n_shard, rows_here, per_chunk * HEAD_DIM)
    attended = jnp.transpose(gathered, (0, 2, 1, 3)).reshape(n_grp * rows_here, -1)

    mean_square = jnp.mean(attended * attended, axis=-1, keepdims=True)
    normed_all = (attended * lax.rsqrt(mean_square + 1e-05) * attn_gain).astype(jnp.bfloat16)
    normed = lax.dynamic_slice_in_dim(normed_all, grp_id * rows_here, rows_here, 0)

    logits = jnp.dot(normed_all, router, preferred_element_type=jnp.float32)
    experts = router.shape[1]
    expert_range = jnp.arange(experts, dtype=jnp.int32)
    expert_hit = expert_ids[:, :, None] == expert_range[None, None, :]
    chosen = jnp.sum(jnp.where(expert_hit, logits[:, None, :], 0.0), axis=-1)
    first_weight = jax.nn.sigmoid(chosen[:, 0] - chosen[:, 1])
    route_weight = jnp.stack([first_weight, 1.0 - first_weight], axis=1)

    local_experts = w_gate.shape[0]
    assert local_experts == 1
    width = normed_all.shape[1]
    total = jnp.zeros((n_grp * rows_here, width), jnp.float32)
    for local in range(local_experts):
        expert_index = grp_id * local_experts + local
        coefficient = jnp.sum(jnp.where(expert_ids == expert_index, route_weight, 0.0), axis=-1)
        gate_proj = jnp.dot(normed_all, w_gate[local], preferred_element_type=jnp.float32)
        up_proj = jnp.dot(normed_all, w_up[local], preferred_element_type=jnp.float32)
        hidden = (jax.nn.silu(gate_proj) * up_proj).astype(jnp.bfloat16)
        expert_y = jnp.dot(hidden, w_down[local], preferred_element_type=jnp.float32)
        total = total + coefficient[:, None] * expert_y

    out_width = width // n_shard
    sending = slot_match(expert_ids, (grp_id * local_experts)[None], rows_here, n_grp)[0]
    grouped = total.reshape(n_grp, 1, rows_here, width)
    picked = jnp.sum(jnp.where(sending[..., None], grouped, 0.0), axis=2)
    blocks = picked.reshape(n_grp, CAP, n_shard, out_width)
    blocks = jnp.transpose(blocks, (0, 2, 1, 3)).reshape(n_dev, CAP, out_width)
    arrived = lax.all_to_all(blocks.astype(jnp.bfloat16), ("grp", "shard"), 0, 0, tiled=True)
    arrived = arrived.astype(jnp.float32)
    per_expert = jnp.sum(arrived.reshape(n_grp, n_shard, CAP, out_width), axis=1)
    own_ids = lax.dynamic_slice_in_dim(expert_ids, grp_id * rows_here, rows_here, 0)
    homes = slot_match(own_ids, jnp.arange(n_grp, dtype=jnp.int32) * local_experts, rows_here, 1)[:, 0]
    spread_back = jnp.where(homes[..., None], per_expert[:, :, None, :], 0.0)
    result = jnp.sum(spread_back, axis=(0, 1))
    return (normed, result.astype(jnp.bfloat16))


def solution(mesh):
    in_specs = (
        P("grp", None),
        P("grp", "shard", None),
        P("grp", "shard", None),
        P("grp"),
        P(),
        P(),
        P(),
        P("grp", None, "shard"),
        P("grp", None, "shard"),
        P("grp", "shard", None),
    )
    out_specs = (P("grp", None), P("grp", "shard"))
    return jax.shard_map(shards, mesh=mesh, in_specs=in_specs, out_specs=out_specs, check_vma=False)
```

```python
import math

import jax
import jax.numpy as jnp
from jax import lax
from jax.experimental import pallas as pl
from jax.experimental.pallas import tpu as pltpu
from jax.sharding import PartitionSpec as P

HEADS = 48
KV_HEADS = 8
HEAD_DIM = 128
BLOCK = 256


NEG_FILL = -1e30
CAP = 2


FF_TILE = 256


def expert_kernel(x_ref, gate_ref, up_ref, down_ref, coef_ref, out_ref, acc_ref):
    step = pl.program_id(0)

    @pl.when(step == 0)
    def _():
        acc_ref[...] = jnp.zeros_like(acc_ref)

    rows = x_ref[...]
    gate_proj = jnp.dot(rows, gate_ref[...], preferred_element_type=jnp.float32)
    up_proj = jnp.dot(rows, up_ref[...], preferred_element_type=jnp.float32)
    hidden = (jax.nn.silu(gate_proj) * up_proj).astype(jnp.bfloat16)
    acc_ref[...] += jnp.dot(hidden, down_ref[...], preferred_element_type=jnp.float32)

    @pl.when(step == pl.num_programs(0) - 1)
    def _():
        out_ref[...] = acc_ref[...] * coef_ref[...]


def expert_ffn(rows, w_gate, w_up, w_down, local, coefficient):
    n_rows, width = rows.shape
    hidden_units = w_gate.shape[2]
    tile = min(FF_TILE, hidden_units)
    return pl.pallas_call(
        expert_kernel,
        grid=(hidden_units // tile,),
        in_specs=[
            pl.BlockSpec((n_rows, width), lambda f: (0, 0)),
            pl.BlockSpec((None, width, tile), lambda f: (local, 0, f)),
            pl.BlockSpec((None, width, tile), lambda f: (local, 0, f)),
            pl.BlockSpec((None, tile, width), lambda f: (local, f, 0)),
            pl.BlockSpec((n_rows, 1), lambda f: (0, 0)),
        ],
        out_specs=pl.BlockSpec((n_rows, width), lambda f: (0, 0)),
        out_shape=jax.ShapeDtypeStruct((n_rows, width), jnp.float32),
        scratch_shapes=[pltpu.VMEM((n_rows, width), jnp.float32)],
        compiler_params=pltpu.CompilerParams(vmem_limit_bytes=48 * 1024 * 1024),
    )(rows, w_gate, w_up, w_down, coefficient[:, None])


def slot_match(expert_ids, experts, rows_here, n_groups):
    ids = expert_ids.reshape(n_groups, rows_here, expert_ids.shape[1])
    hit = jnp.any(ids[None, :, :, :] == experts[:, None, None, None], axis=-1)
    rank = jnp.cumsum(hit.astype(jnp.int32), axis=-1) - 1
    slot = jnp.arange(CAP, dtype=jnp.int32)
    return hit[:, :, None, :] & (rank[:, :, None, :] == slot[None, None, :, None])


def shards(
    query_rows, key_cache, value_cache, lengths, attn_gain, router, expert_ids, w_gate, w_up, w_down
):
    rows_here = query_rows.shape[0]
    span = key_cache.shape[1]
    kv_share = HEADS // KV_HEADS
    n_grp = lax.axis_size("grp")
    n_shard = lax.axis_size("shard")
    grp_id = lax.axis_index("grp")
    shard_id = lax.axis_index("shard")
    n_blocks = span // BLOCK

    query_heads = query_rows.reshape(rows_here, KV_HEADS, kv_share, HEAD_DIM)
    key_heads = key_cache.reshape(rows_here, span, KV_HEADS, HEAD_DIM)
    value_heads = value_cache.reshape(rows_here, n_blocks, BLOCK, KV_HEADS, HEAD_DIM)
    scores = jnp.einsum(
        "rgjd,rtgd->rgjt", query_heads, key_heads, preferred_element_type=jnp.float32
    ) / math.sqrt(HEAD_DIM)
    position = shard_id * span + jnp.arange(span, dtype=jnp.int32)
    live_mask = (position[None, :] < lengths[:, None])[:, None, None, :]
    scores = jnp.where(live_mask, scores, NEG_FILL)
    scores = scores.reshape(rows_here, KV_HEADS, kv_share, n_blocks, BLOCK)
    live_blocks = live_mask.reshape(rows_here, 1, 1, n_blocks, BLOCK)
    block_max = jnp.max(scores, axis=-1)
    block_probs = jnp.where(live_blocks, jnp.exp(scores - block_max[..., None]), 0.0).astype(
        jnp.bfloat16
    )
    block_sum = jnp.sum(block_probs.astype(jnp.float32), axis=-1)
    block_mix = jnp.einsum(
        "rgjbt,rbtgd->rgjbd", block_probs, value_heads, preferred_element_type=jnp.float32
    )
    dev_max = jnp.max(block_max, axis=-1)
    dev_factor = jnp.exp(block_max - dev_max[..., None])
    dev_sum = jnp.sum(block_sum * dev_factor, axis=-1).reshape(rows_here, HEADS)
    dev_mix = jnp.sum(block_mix * dev_factor[..., None], axis=-2).reshape(rows_here, HEADS, HEAD_DIM)
    dev_max = dev_max.reshape(rows_here, HEADS)

    per_chunk = HEADS // n_shard
    mix_out = dev_mix.reshape(rows_here, n_shard, per_chunk, HEAD_DIM)
    side = jnp.concatenate(
        [dev_max.reshape(rows_here, n_shard, per_chunk), dev_sum.reshape(rows_here, n_shard, per_chunk)],
        axis=-1,
    )
    side = jnp.pad(side, ((0, 0), (0, 0), (0, HEAD_DIM - 2 * per_chunk)))
    packed = jnp.concatenate([mix_out, side[:, :, None, :]], axis=2)
    packed = jnp.transpose(packed, (1, 0, 2, 3))
    stats = lax.all_to_all(packed, "shard", 0, 0, tiled=True)
    got_mix = stats[:, :, :per_chunk, :]
    got_max = stats[:, :, per_chunk, :per_chunk]
    got_sum = stats[:, :, per_chunk, per_chunk : 2 * per_chunk]
    top = jnp.max(got_max, axis=0)
    factor = jnp.exp(got_max - top[None])
    whole_sum = jnp.sum(got_sum * factor, axis=0)
    whole_mix = jnp.sum(got_mix * factor[..., None], axis=0)
    chunk = (whole_mix / whole_sum[..., None]).reshape(rows_here, per_chunk * HEAD_DIM)

    n_dev = n_grp * n_shard
    spread = jnp.broadcast_to(chunk.astype(jnp.bfloat16)[None], (n_dev,) + chunk.shape)
    gathered = lax.all_to_all(spread, ("grp", "shard"), 0, 0, tiled=True).astype(jnp.float32)
    gathered = gathered.reshape(n_grp, n_shard, rows_here, per_chunk * HEAD_DIM)
    attended = jnp.transpose(gathered, (0, 2, 1, 3)).reshape(n_grp * rows_here, -1)

    mean_square = jnp.mean(attended * attended, axis=-1, keepdims=True)
    normed_all = (attended * lax.rsqrt(mean_square + 1e-05) * attn_gain).astype(jnp.bfloat16)
    normed = lax.dynamic_slice_in_dim(normed_all, grp_id * rows_here, rows_here, 0)

    logits = jnp.dot(normed_all, router, preferred_element_type=jnp.float32)
    experts = router.shape[1]
    expert_range = jnp.arange(experts, dtype=jnp.int32)
    expert_hit = expert_ids[:, :, None] == expert_range[None, None, :]
    chosen = jnp.sum(jnp.where(expert_hit, logits[:, None, :], 0.0), axis=-1)
    first_weight = jax.nn.sigmoid(chosen[:, 0] - chosen[:, 1])
    route_weight = jnp.stack([first_weight, 1.0 - first_weight], axis=1)

    local_experts = w_gate.shape[0]
    assert local_experts == 1
    width = normed_all.shape[1]
    total = None
    for local in range(local_experts):
        expert_index = grp_id * local_experts + local
        coefficient = jnp.sum(jnp.where(expert_ids == expert_index, route_weight, 0.0), axis=-1)
        contribution = expert_ffn(normed_all, w_gate, w_up, w_down, local, coefficient)
        total = contribution if total is None else total + contribution

    out_width = width // n_shard
    sending = slot_match(expert_ids, (grp_id * local_experts)[None], rows_here, n_grp)[0]
    grouped = total.reshape(n_grp, 1, rows_here, width)
    picked = jnp.sum(jnp.where(sending[..., None], grouped, 0.0), axis=2)
    blocks = picked.reshape(n_grp, CAP, n_shard, out_width)
    blocks = jnp.transpose(blocks, (0, 2, 1, 3)).reshape(n_dev, CAP, out_width)
    arrived = lax.all_to_all(blocks.astype(jnp.bfloat16), ("grp", "shard"), 0, 0, tiled=True)
    arrived = arrived.astype(jnp.float32)
    per_expert = jnp.sum(arrived.reshape(n_grp, n_shard, CAP, out_width), axis=1)
    own_ids = lax.dynamic_slice_in_dim(expert_ids, grp_id * rows_here, rows_here, 0)
    homes = slot_match(own_ids, jnp.arange(n_grp, dtype=jnp.int32) * local_experts, rows_here, 1)[:, 0]
    spread_back = jnp.where(homes[..., None], per_expert[:, :, None, :], 0.0)
    result = jnp.sum(spread_back, axis=(0, 1))
    return (normed, result.astype(jnp.bfloat16))


def solution(mesh):
    in_specs = (
        P("grp", None),
        P("grp", "shard", None),
        P("grp", "shard", None),
        P("grp"),
        P(),
        P(),
        P(),
        P("grp", None, "shard"),
        P("grp", None, "shard"),
        P("grp", "shard", None),
    )
    out_specs = (P("grp", None), P("grp", "shard"))
    return jax.shard_map(shards, mesh=mesh, in_specs=in_specs, out_specs=out_specs, check_vma=False)
```

```python
import math

import jax
import jax.numpy as jnp
from jax import lax
from jax.experimental import pallas as pl
from jax.experimental.pallas import tpu as pltpu
from jax.sharding import PartitionSpec as P

HEADS = 48
KV_HEADS = 8
HEAD_DIM = 128
BLOCK = 256


NEG_FILL = -1e30
CAP = 2


FF_TILE = 256


def expert_kernel(x_ref, gate_ref, up_ref, down_ref, sel_ref, out_ref, acc_ref):
    step = pl.program_id(0)

    @pl.when(step == 0)
    def _():
        acc_ref[...] = jnp.zeros_like(acc_ref)

    rows = x_ref[...]
    gate_proj = jnp.dot(rows, gate_ref[...], preferred_element_type=jnp.float32)
    up_proj = jnp.dot(rows, up_ref[...], preferred_element_type=jnp.float32)
    hidden = (jax.nn.silu(gate_proj) * up_proj).astype(jnp.bfloat16)
    acc_ref[...] += jnp.dot(hidden, down_ref[...], preferred_element_type=jnp.float32)

    @pl.when(step == pl.num_programs(0) - 1)
    def _():
        picked = jnp.dot(
            sel_ref[...], acc_ref[...], precision=lax.Precision.HIGHEST,
            preferred_element_type=jnp.float32,
        )
        out_ref[...] = picked.astype(out_ref.dtype)


def expert_ffn(rows, w_gate, w_up, w_down, local, select):
    n_rows, width = rows.shape
    n_out = select.shape[0]
    hidden_units = w_gate.shape[2]
    tile = min(FF_TILE, hidden_units)
    return pl.pallas_call(
        expert_kernel,
        grid=(hidden_units // tile,),
        in_specs=[
            pl.BlockSpec((n_rows, width), lambda f: (0, 0)),
            pl.BlockSpec((None, width, tile), lambda f: (local, 0, f)),
            pl.BlockSpec((None, width, tile), lambda f: (local, 0, f)),
            pl.BlockSpec((None, tile, width), lambda f: (local, f, 0)),
            pl.BlockSpec((n_out, n_rows), lambda f: (0, 0)),
        ],
        out_specs=pl.BlockSpec((n_out, width), lambda f: (0, 0)),
        out_shape=jax.ShapeDtypeStruct((n_out, width), jnp.bfloat16),
        scratch_shapes=[pltpu.VMEM((n_rows, width), jnp.float32)],
        compiler_params=pltpu.CompilerParams(vmem_limit_bytes=48 * 1024 * 1024),
    )(rows, w_gate, w_up, w_down, select)


def slot_match(expert_ids, experts, rows_here, n_groups):
    ids = expert_ids.reshape(n_groups, rows_here, expert_ids.shape[1])
    hit = jnp.any(ids[None, :, :, :] == experts[:, None, None, None], axis=-1)
    rank = jnp.cumsum(hit.astype(jnp.int32), axis=-1) - 1
    slot = jnp.arange(CAP, dtype=jnp.int32)
    return hit[:, :, None, :] & (rank[:, :, None, :] == slot[None, None, :, None])


def shards(
    query_rows, key_cache, value_cache, lengths, attn_gain, router, expert_ids, w_gate, w_up, w_down
):
    rows_here = query_rows.shape[0]
    span = key_cache.shape[1]
    kv_share = HEADS // KV_HEADS
    n_grp = lax.axis_size("grp")
    n_shard = lax.axis_size("shard")
    grp_id = lax.axis_index("grp")
    shard_id = lax.axis_index("shard")
    n_blocks = span // BLOCK

    query_heads = query_rows.reshape(rows_here, KV_HEADS, kv_share, HEAD_DIM)
    key_heads = key_cache.reshape(rows_here, span, KV_HEADS, HEAD_DIM)
    value_heads = value_cache.reshape(rows_here, n_blocks, BLOCK, KV_HEADS, HEAD_DIM)
    scores = jnp.einsum(
        "rgjd,rtgd->rgjt", query_heads, key_heads, preferred_element_type=jnp.float32
    ) / math.sqrt(HEAD_DIM)
    position = shard_id * span + jnp.arange(span, dtype=jnp.int32)
    live_mask = (position[None, :] < lengths[:, None])[:, None, None, :]
    scores = jnp.where(live_mask, scores, NEG_FILL)
    scores = scores.reshape(rows_here, KV_HEADS, kv_share, n_blocks, BLOCK)
    live_blocks = live_mask.reshape(rows_here, 1, 1, n_blocks, BLOCK)
    block_max = jnp.max(scores, axis=-1)
    block_probs = jnp.where(live_blocks, jnp.exp(scores - block_max[..., None]), 0.0).astype(
        jnp.bfloat16
    )
    block_sum = jnp.sum(block_probs.astype(jnp.float32), axis=-1)
    block_mix = jnp.einsum(
        "rgjbt,rbtgd->rgjbd", block_probs, value_heads, preferred_element_type=jnp.float32
    )
    dev_max = jnp.max(block_max, axis=-1)
    dev_factor = jnp.exp(block_max - dev_max[..., None])
    dev_sum = jnp.sum(block_sum * dev_factor, axis=-1).reshape(rows_here, HEADS)
    dev_mix = jnp.sum(block_mix * dev_factor[..., None], axis=-2).reshape(rows_here, HEADS, HEAD_DIM)
    dev_max = dev_max.reshape(rows_here, HEADS)

    per_chunk = HEADS // n_shard
    mix_out = dev_mix.reshape(rows_here, n_shard, per_chunk, HEAD_DIM)
    side = jnp.concatenate(
        [dev_max.reshape(rows_here, n_shard, per_chunk), dev_sum.reshape(rows_here, n_shard, per_chunk)],
        axis=-1,
    )
    side = jnp.pad(side, ((0, 0), (0, 0), (0, HEAD_DIM - 2 * per_chunk)))
    packed = jnp.concatenate([mix_out, side[:, :, None, :]], axis=2)
    packed = jnp.transpose(packed, (1, 0, 2, 3))
    stats = lax.all_to_all(packed, "shard", 0, 0, tiled=True)
    got_mix = stats[:, :, :per_chunk, :]
    got_max = stats[:, :, per_chunk, :per_chunk]
    got_sum = stats[:, :, per_chunk, per_chunk : 2 * per_chunk]
    top = jnp.max(got_max, axis=0)
    factor = jnp.exp(got_max - top[None])
    whole_sum = jnp.sum(got_sum * factor, axis=0)
    whole_mix = jnp.sum(got_mix * factor[..., None], axis=0)
    chunk = (whole_mix / whole_sum[..., None]).reshape(rows_here, per_chunk * HEAD_DIM)

    n_dev = n_grp * n_shard
    spread = jnp.broadcast_to(chunk.astype(jnp.bfloat16)[None], (n_dev,) + chunk.shape)
    gathered = lax.all_to_all(spread, ("grp", "shard"), 0, 0, tiled=True).astype(jnp.float32)
    gathered = gathered.reshape(n_grp, n_shard, rows_here, per_chunk * HEAD_DIM)
    attended = jnp.transpose(gathered, (0, 2, 1, 3)).reshape(n_grp * rows_here, -1)

    mean_square = jnp.mean(attended * attended, axis=-1, keepdims=True)
    normed_all = (attended * lax.rsqrt(mean_square + 1e-05) * attn_gain).astype(jnp.bfloat16)
    normed = lax.dynamic_slice_in_dim(normed_all, grp_id * rows_here, rows_here, 0)

    logits = jnp.dot(normed_all, router, preferred_element_type=jnp.float32)
    experts = router.shape[1]
    expert_range = jnp.arange(experts, dtype=jnp.int32)
    expert_hit = expert_ids[:, :, None] == expert_range[None, None, :]
    chosen = jnp.sum(jnp.where(expert_hit, logits[:, None, :], 0.0), axis=-1)
    first_weight = jax.nn.sigmoid(chosen[:, 0] - chosen[:, 1])
    route_weight = jnp.stack([first_weight, 1.0 - first_weight], axis=1)

    local_experts = w_gate.shape[0]
    assert local_experts == 1
    width = normed_all.shape[1]
    out_width = width // n_shard
    expert_index = grp_id
    coefficient = jnp.sum(jnp.where(expert_ids == expert_index, route_weight, 0.0), axis=-1)
    sending = slot_match(expert_ids, expert_index[None], rows_here, n_grp)[0]
    row_of = jnp.arange(n_grp * rows_here, dtype=jnp.int32).reshape(n_grp, 1, rows_here)
    select = jnp.sum(
        jnp.where(
            sending[..., None] & (row_of[..., None] == jnp.arange(n_grp * rows_here)[None, None, None, :]),
            coefficient[None, None, None, :],
            0.0,
        ),
        axis=2,
    )
    select = jnp.transpose(select, (1, 0, 2)).reshape(CAP * n_grp, n_grp * rows_here)
    picked = expert_ffn(normed_all, w_gate, w_up, w_down, 0, select)
    blocks = picked.reshape(CAP, n_dev, out_width)
    arrived = lax.all_to_all(blocks, ("grp", "shard"), 1, 1, tiled=True)
    arrived = arrived.astype(jnp.float32).reshape(CAP, n_grp, n_shard, out_width)
    per_expert = jnp.transpose(jnp.sum(arrived, axis=2), (1, 0, 2))
    own_ids = lax.dynamic_slice_in_dim(expert_ids, grp_id * rows_here, rows_here, 0)
    homes = slot_match(own_ids, jnp.arange(n_grp, dtype=jnp.int32) * local_experts, rows_here, 1)[:, 0]
    spread_back = jnp.where(homes[..., None], per_expert[:, :, None, :], 0.0)
    result = jnp.sum(spread_back, axis=(0, 1))
    return (normed, result.astype(jnp.bfloat16))


def solution(mesh):
    in_specs = (
        P("grp", None),
        P("grp", "shard", None),
        P("grp", "shard", None),
        P("grp"),
        P(),
        P(),
        P(),
        P("grp", None, "shard"),
        P("grp", None, "shard"),
        P("grp", "shard", None),
    )
    out_specs = (P("grp", None), P("grp", "shard"))
    return jax.shard_map(shards, mesh=mesh, in_specs=in_specs, out_specs=out_specs, check_vma=False)
```

```python
import math

import jax
import jax.numpy as jnp
from jax import lax
from jax.experimental import pallas as pl
from jax.experimental.pallas import tpu as pltpu
from jax.sharding import PartitionSpec as P

HEADS = 48
KV_HEADS = 8
HEAD_DIM = 128
BLOCK = 256


NEG_FILL = -1e30
CAP = 2


FF_TILE = 256


def expert_kernel(x_ref, gate_ref, up_ref, down_ref, sel_ref, out_ref, acc_ref):
    step = pl.program_id(0)

    @pl.when(step == 0)
    def _():
        acc_ref[...] = jnp.zeros_like(acc_ref)

    rows = x_ref[...]
    gate_proj = jnp.dot(rows, gate_ref[...], preferred_element_type=jnp.float32)
    up_proj = jnp.dot(rows, up_ref[...], preferred_element_type=jnp.float32)
    hidden = (jax.nn.silu(gate_proj) * up_proj).astype(jnp.bfloat16)
    acc_ref[...] += jnp.dot(hidden, down_ref[...], preferred_element_type=jnp.float32)

    @pl.when(step == pl.num_programs(0) - 1)
    def _():
        picked = jnp.dot(
            sel_ref[...], acc_ref[...], precision=lax.Precision.HIGHEST,
            preferred_element_type=jnp.float32,
        ).astype(out_ref.dtype)
        n_dev, slots, out_width = out_ref.shape
        n_groups = sel_ref.shape[0] // slots
        n_cols = n_dev // n_groups
        for slot in range(slots):
            for group in range(n_groups):
                for col in range(n_cols):
                    out_ref[group * n_cols + col, slot, :] = picked[
                        slot * n_groups + group, col * out_width : (col + 1) * out_width
                    ]


def expert_ffn(rows, w_gate, w_up, w_down, local, select, n_dev):
    n_rows, width = rows.shape
    slots = CAP
    out_width = width * select.shape[0] // (slots * n_dev)
    hidden_units = w_gate.shape[2]
    tile = min(FF_TILE, hidden_units)
    return pl.pallas_call(
        expert_kernel,
        grid=(hidden_units // tile,),
        in_specs=[
            pl.BlockSpec((n_rows, width), lambda f: (0, 0)),
            pl.BlockSpec((None, width, tile), lambda f: (local, 0, f)),
            pl.BlockSpec((None, width, tile), lambda f: (local, 0, f)),
            pl.BlockSpec((None, tile, width), lambda f: (local, f, 0)),
            pl.BlockSpec(select.shape, lambda f: (0, 0)),
        ],
        out_specs=pl.BlockSpec((n_dev, slots, out_width), lambda f: (0, 0, 0)),
        out_shape=jax.ShapeDtypeStruct((n_dev, slots, out_width), jnp.bfloat16),
        scratch_shapes=[pltpu.VMEM((n_rows, width), jnp.float32)],
        compiler_params=pltpu.CompilerParams(vmem_limit_bytes=48 * 1024 * 1024),
    )(rows, w_gate, w_up, w_down, select)


def slot_match(expert_ids, experts, rows_here, n_groups):
    ids = expert_ids.reshape(n_groups, rows_here, expert_ids.shape[1])
    hit = jnp.any(ids[None, :, :, :] == experts[:, None, None, None], axis=-1)
    rank = jnp.cumsum(hit.astype(jnp.int32), axis=-1) - 1
    slot = jnp.arange(CAP, dtype=jnp.int32)
    return hit[:, :, None, :] & (rank[:, :, None, :] == slot[None, None, :, None])


def shards(
    query_rows, key_cache, value_cache, lengths, attn_gain, router, expert_ids, w_gate, w_up, w_down
):
    rows_here = query_rows.shape[0]
    span = key_cache.shape[1]
    kv_share = HEADS // KV_HEADS
    n_grp = lax.axis_size("grp")
    n_shard = lax.axis_size("shard")
    grp_id = lax.axis_index("grp")
    shard_id = lax.axis_index("shard")
    n_blocks = span // BLOCK

    query_heads = query_rows.reshape(rows_here, KV_HEADS, kv_share, HEAD_DIM)
    key_heads = key_cache.reshape(rows_here, span, KV_HEADS, HEAD_DIM)
    value_heads = value_cache.reshape(rows_here, n_blocks, BLOCK, KV_HEADS, HEAD_DIM)
    scores = jnp.einsum(
        "rgjd,rtgd->rgjt", query_heads, key_heads, preferred_element_type=jnp.float32
    ) / math.sqrt(HEAD_DIM)
    position = shard_id * span + jnp.arange(span, dtype=jnp.int32)
    live_mask = (position[None, :] < lengths[:, None])[:, None, None, :]
    scores = jnp.where(live_mask, scores, NEG_FILL)
    scores = scores.reshape(rows_here, KV_HEADS, kv_share, n_blocks, BLOCK)
    live_blocks = live_mask.reshape(rows_here, 1, 1, n_blocks, BLOCK)
    block_max = jnp.max(scores, axis=-1)
    block_probs = jnp.where(live_blocks, jnp.exp(scores - block_max[..., None]), 0.0).astype(
        jnp.bfloat16
    )
    block_sum = jnp.sum(block_probs.astype(jnp.float32), axis=-1)
    block_mix = jnp.einsum(
        "rgjbt,rbtgd->rgjbd", block_probs, value_heads, preferred_element_type=jnp.float32
    )
    dev_max = jnp.max(block_max, axis=-1)
    dev_factor = jnp.exp(block_max - dev_max[..., None])
    dev_sum = jnp.sum(block_sum * dev_factor, axis=-1).reshape(rows_here, HEADS)
    dev_mix = jnp.sum(block_mix * dev_factor[..., None], axis=-2).reshape(rows_here, HEADS, HEAD_DIM)
    dev_max = dev_max.reshape(rows_here, HEADS)

    per_chunk = HEADS // n_shard
    mix_out = dev_mix.reshape(rows_here, n_shard, per_chunk, HEAD_DIM)
    side = jnp.concatenate(
        [dev_max.reshape(rows_here, n_shard, per_chunk), dev_sum.reshape(rows_here, n_shard, per_chunk)],
        axis=-1,
    )
    side = jnp.pad(side, ((0, 0), (0, 0), (0, HEAD_DIM - 2 * per_chunk)))
    packed = jnp.concatenate([mix_out, side[:, :, None, :]], axis=2)
    packed = jnp.transpose(packed, (1, 0, 2, 3))
    stats = lax.all_to_all(packed, "shard", 0, 0, tiled=True)
    got_mix = stats[:, :, :per_chunk, :]
    got_max = stats[:, :, per_chunk, :per_chunk]
    got_sum = stats[:, :, per_chunk, per_chunk : 2 * per_chunk]
    top = jnp.max(got_max, axis=0)
    factor = jnp.exp(got_max - top[None])
    whole_sum = jnp.sum(got_sum * factor, axis=0)
    whole_mix = jnp.sum(got_mix * factor[..., None], axis=0)
    chunk = (whole_mix / whole_sum[..., None]).reshape(rows_here, per_chunk * HEAD_DIM)

    n_dev = n_grp * n_shard
    spread = jnp.broadcast_to(chunk.astype(jnp.bfloat16)[None], (n_dev,) + chunk.shape)
    gathered = lax.all_to_all(spread, ("grp", "shard"), 0, 0, tiled=True).astype(jnp.float32)
    gathered = gathered.reshape(n_grp, n_shard, rows_here, per_chunk * HEAD_DIM)
    attended = jnp.transpose(gathered, (0, 2, 1, 3)).reshape(n_grp * rows_here, -1)

    mean_square = jnp.mean(attended * attended, axis=-1, keepdims=True)
    normed_all = (attended * lax.rsqrt(mean_square + 1e-05) * attn_gain).astype(jnp.bfloat16)
    normed = lax.dynamic_slice_in_dim(normed_all, grp_id * rows_here, rows_here, 0)

    logits = jnp.dot(normed_all, router, preferred_element_type=jnp.float32)
    experts = router.shape[1]
    expert_range = jnp.arange(experts, dtype=jnp.int32)
    expert_hit = expert_ids[:, :, None] == expert_range[None, None, :]
    chosen = jnp.sum(jnp.where(expert_hit, logits[:, None, :], 0.0), axis=-1)
    first_weight = jax.nn.sigmoid(chosen[:, 0] - chosen[:, 1])
    route_weight = jnp.stack([first_weight, 1.0 - first_weight], axis=1)

    local_experts = w_gate.shape[0]
    assert local_experts == 1
    width = normed_all.shape[1]
    out_width = width // n_shard
    expert_index = grp_id
    coefficient = jnp.sum(jnp.where(expert_ids == expert_index, route_weight, 0.0), axis=-1)
    sending = slot_match(expert_ids, expert_index[None], rows_here, n_grp)[0]
    row_of = jnp.arange(n_grp * rows_here, dtype=jnp.int32).reshape(n_grp, 1, rows_here)
    select = jnp.sum(
        jnp.where(
            sending[..., None] & (row_of[..., None] == jnp.arange(n_grp * rows_here)[None, None, None, :]),
            coefficient[None, None, None, :],
            0.0,
        ),
        axis=2,
    )
    select = jnp.transpose(select, (1, 0, 2)).reshape(CAP * n_grp, n_grp * rows_here)
    blocks = expert_ffn(normed_all, w_gate, w_up, w_down, 0, select, n_dev)
    arrived = lax.all_to_all(blocks, ("grp", "shard"), 0, 0, tiled=True)
    arrived = arrived.astype(jnp.float32).reshape(n_grp, n_shard, CAP, out_width)
    per_expert = jnp.sum(arrived, axis=1)
    own_ids = lax.dynamic_slice_in_dim(expert_ids, grp_id * rows_here, rows_here, 0)
    homes = slot_match(own_ids, jnp.arange(n_grp, dtype=jnp.int32) * local_experts, rows_here, 1)[:, 0]
    spread_back = jnp.where(homes[..., None], per_expert[:, :, None, :], 0.0)
    result = jnp.sum(spread_back, axis=(0, 1))
    return (normed, result.astype(jnp.bfloat16))


def solution(mesh):
    in_specs = (
        P("grp", None),
        P("grp", "shard", None),
        P("grp", "shard", None),
        P("grp"),
        P(),
        P(),
        P(),
        P("grp", None, "shard"),
        P("grp", None, "shard"),
        P("grp", "shard", None),
    )
    out_specs = (P("grp", None), P("grp", "shard"))
    return jax.shard_map(shards, mesh=mesh, in_specs=in_specs, out_specs=out_specs, check_vma=False)
```

```python
import math

import jax
import jax.numpy as jnp
from jax import lax
from jax.experimental import pallas as pl
from jax.experimental.pallas import tpu as pltpu
from jax.sharding import PartitionSpec as P

HEADS = 48
KV_HEADS = 8
HEAD_DIM = 128
BLOCK = 256


NEG_FILL = -1e30
CAP = 2


FF_TILE = 256


def expert_kernel(x_ref, gate_ref, up_ref, down_ref, sel_ref, out_ref, acc_ref):
    step = pl.program_id(0)
    n_cols, _, out_width = acc_ref.shape
    n_sel = sel_ref.shape[0]

    @pl.when(step == 0)
    def _():
        acc_ref[...] = jnp.zeros_like(acc_ref)

    rows = x_ref[...]
    gate_proj = jnp.dot(rows, gate_ref[...], preferred_element_type=jnp.float32)
    up_proj = jnp.dot(rows, up_ref[...], preferred_element_type=jnp.float32)
    hidden = (jax.nn.silu(gate_proj) * up_proj).astype(jnp.bfloat16)
    for col in range(n_cols):
        acc_ref[col] += jnp.dot(
            hidden, down_ref[:, col * out_width : (col + 1) * out_width],
            preferred_element_type=jnp.float32,
        )

    @pl.when(step == pl.num_programs(0) - 1)
    def _():
        for col in range(n_cols):
            picked = jnp.dot(
                sel_ref[...], acc_ref[col], precision=lax.Precision.HIGHEST,
                preferred_element_type=jnp.float32,
            )
            out_ref[col * n_sel : (col + 1) * n_sel, :] = picked.astype(out_ref.dtype)


def expert_ffn(rows, w_gate, w_up, w_down, local, select, n_cols):
    n_rows, width = rows.shape
    n_sel = select.shape[0]
    out_width = width // n_cols
    hidden_units = w_gate.shape[2]
    tile = min(FF_TILE, hidden_units)
    return pl.pallas_call(
        expert_kernel,
        grid=(hidden_units // tile,),
        in_specs=[
            pl.BlockSpec((n_rows, width), lambda f: (0, 0)),
            pl.BlockSpec((None, width, tile), lambda f: (local, 0, f)),
            pl.BlockSpec((None, width, tile), lambda f: (local, 0, f)),
            pl.BlockSpec((None, tile, width), lambda f: (local, f, 0)),
            pl.BlockSpec(select.shape, lambda f: (0, 0)),
        ],
        out_specs=pl.BlockSpec((n_cols * n_sel, out_width), lambda f: (0, 0)),
        out_shape=jax.ShapeDtypeStruct((n_cols * n_sel, out_width), jnp.bfloat16),
        scratch_shapes=[pltpu.VMEM((n_cols, n_rows, out_width), jnp.float32)],
        compiler_params=pltpu.CompilerParams(vmem_limit_bytes=48 * 1024 * 1024),
    )(rows, w_gate, w_up, w_down, select)


def slot_match(expert_ids, experts, rows_here, n_groups):
    ids = expert_ids.reshape(n_groups, rows_here, expert_ids.shape[1])
    hit = jnp.any(ids[None, :, :, :] == experts[:, None, None, None], axis=-1)
    rank = jnp.cumsum(hit.astype(jnp.int32), axis=-1) - 1
    slot = jnp.arange(CAP, dtype=jnp.int32)
    return hit[:, :, None, :] & (rank[:, :, None, :] == slot[None, None, :, None])


def shards(
    query_rows, key_cache, value_cache, lengths, attn_gain, router, expert_ids, w_gate, w_up, w_down
):
    rows_here = query_rows.shape[0]
    span = key_cache.shape[1]
    kv_share = HEADS // KV_HEADS
    n_grp = lax.axis_size("grp")
    n_shard = lax.axis_size("shard")
    grp_id = lax.axis_index("grp")
    shard_id = lax.axis_index("shard")
    n_blocks = span // BLOCK

    query_heads = query_rows.reshape(rows_here, KV_HEADS, kv_share, HEAD_DIM)
    key_heads = key_cache.reshape(rows_here, span, KV_HEADS, HEAD_DIM)
    value_heads = value_cache.reshape(rows_here, n_blocks, BLOCK, KV_HEADS, HEAD_DIM)
    scores = jnp.einsum(
        "rgjd,rtgd->rgjt", query_heads, key_heads, preferred_element_type=jnp.float32
    ) / math.sqrt(HEAD_DIM)
    position = shard_id * span + jnp.arange(span, dtype=jnp.int32)
    live_mask = (position[None, :] < lengths[:, None])[:, None, None, :]
    scores = jnp.where(live_mask, scores, NEG_FILL)
    scores = scores.reshape(rows_here, KV_HEADS, kv_share, n_blocks, BLOCK)
    live_blocks = live_mask.reshape(rows_here, 1, 1, n_blocks, BLOCK)
    block_max = jnp.max(scores, axis=-1)
    block_probs = jnp.where(live_blocks, jnp.exp(scores - block_max[..., None]), 0.0).astype(
        jnp.bfloat16
    )
    block_sum = jnp.sum(block_probs.astype(jnp.float32), axis=-1)
    block_mix = jnp.einsum(
        "rgjbt,rbtgd->rgjbd", block_probs, value_heads, preferred_element_type=jnp.float32
    )
    dev_max = jnp.max(block_max, axis=-1)
    dev_factor = jnp.exp(block_max - dev_max[..., None])
    dev_sum = jnp.sum(block_sum * dev_factor, axis=-1).reshape(rows_here, HEADS)
    dev_mix = jnp.sum(block_mix * dev_factor[..., None], axis=-2).reshape(rows_here, HEADS, HEAD_DIM)
    dev_max = dev_max.reshape(rows_here, HEADS)

    per_chunk = HEADS // n_shard
    mix_out = dev_mix.reshape(rows_here, n_shard, per_chunk, HEAD_DIM)
    side = jnp.concatenate(
        [dev_max.reshape(rows_here, n_shard, per_chunk), dev_sum.reshape(rows_here, n_shard, per_chunk)],
        axis=-1,
    )
    side = jnp.pad(side, ((0, 0), (0, 0), (0, HEAD_DIM - 2 * per_chunk)))
    packed = jnp.concatenate([mix_out, side[:, :, None, :]], axis=2)
    packed = jnp.transpose(packed, (1, 0, 2, 3))
    stats = lax.all_to_all(packed, "shard", 0, 0, tiled=True)
    got_mix = stats[:, :, :per_chunk, :]
    got_max = stats[:, :, per_chunk, :per_chunk]
    got_sum = stats[:, :, per_chunk, per_chunk : 2 * per_chunk]
    top = jnp.max(got_max, axis=0)
    factor = jnp.exp(got_max - top[None])
    whole_sum = jnp.sum(got_sum * factor, axis=0)
    whole_mix = jnp.sum(got_mix * factor[..., None], axis=0)
    chunk = (whole_mix / whole_sum[..., None]).reshape(rows_here, per_chunk * HEAD_DIM)

    n_dev = n_grp * n_shard
    spread = jnp.broadcast_to(chunk.astype(jnp.bfloat16)[None], (n_dev,) + chunk.shape)
    gathered = lax.all_to_all(spread, ("grp", "shard"), 0, 0, tiled=True).astype(jnp.float32)
    gathered = gathered.reshape(n_grp, n_shard, rows_here, per_chunk * HEAD_DIM)
    attended = jnp.transpose(gathered, (0, 2, 1, 3)).reshape(n_grp * rows_here, -1)

    mean_square = jnp.mean(attended * attended, axis=-1, keepdims=True)
    normed_all = (attended * lax.rsqrt(mean_square + 1e-05) * attn_gain).astype(jnp.bfloat16)
    normed = lax.dynamic_slice_in_dim(normed_all, grp_id * rows_here, rows_here, 0)

    logits = jnp.dot(normed_all, router, preferred_element_type=jnp.float32)
    experts = router.shape[1]
    expert_range = jnp.arange(experts, dtype=jnp.int32)
    expert_hit = expert_ids[:, :, None] == expert_range[None, None, :]
    chosen = jnp.sum(jnp.where(expert_hit, logits[:, None, :], 0.0), axis=-1)
    first_weight = jax.nn.sigmoid(chosen[:, 0] - chosen[:, 1])
    route_weight = jnp.stack([first_weight, 1.0 - first_weight], axis=1)

    local_experts = w_gate.shape[0]
    assert local_experts == 1
    width = normed_all.shape[1]
    out_width = width // n_shard
    expert_index = grp_id
    coefficient = jnp.sum(jnp.where(expert_ids == expert_index, route_weight, 0.0), axis=-1)
    sending = slot_match(expert_ids, expert_index[None], rows_here, n_grp)[0]
    row_of = jnp.arange(n_grp * rows_here, dtype=jnp.int32).reshape(n_grp, 1, rows_here)
    select = jnp.sum(
        jnp.where(
            sending[..., None] & (row_of[..., None] == jnp.arange(n_grp * rows_here)[None, None, None, :]),
            coefficient[None, None, None, :],
            0.0,
        ),
        axis=2,
    )
    select = select.reshape(n_grp * CAP, n_grp * rows_here)
    blocks = expert_ffn(normed_all, w_gate, w_up, w_down, 0, select, n_shard)
    arrived = lax.all_to_all(blocks, ("shard", "grp"), 0, 0, tiled=True)
    arrived = arrived.astype(jnp.float32).reshape(n_shard, n_grp, CAP, out_width)
    per_expert = jnp.sum(arrived, axis=0)
    own_ids = lax.dynamic_slice_in_dim(expert_ids, grp_id * rows_here, rows_here, 0)
    homes = slot_match(own_ids, jnp.arange(n_grp, dtype=jnp.int32) * local_experts, rows_here, 1)[:, 0]
    spread_back = jnp.where(homes[..., None], per_expert[:, :, None, :], 0.0)
    result = jnp.sum(spread_back, axis=(0, 1))
    return (normed, result.astype(jnp.bfloat16))


def solution(mesh):
    in_specs = (
        P("grp", None),
        P("grp", "shard", None),
        P("grp", "shard", None),
        P("grp"),
        P(),
        P(),
        P(),
        P("grp", None, "shard"),
        P("grp", None, "shard"),
        P("grp", "shard", None),
    )
    out_specs = (P("grp", None), P("grp", "shard"))
    return jax.shard_map(shards, mesh=mesh, in_specs=in_specs, out_specs=out_specs, check_vma=False)
```

```python
import math

import jax
import jax.numpy as jnp
from jax import lax
from jax.experimental import pallas as pl
from jax.experimental.pallas import tpu as pltpu
from jax.sharding import PartitionSpec as P

HEADS = 48
KV_HEADS = 8
HEAD_DIM = 128
BLOCK = 256


NEG_FILL = -1e30
CAP = 2


FF_TILE = 256


def expert_kernel(x_ref, gate_ref, up_ref, down_ref, sel_ref, out_ref, acc_ref):
    step = pl.program_id(0)
    n_cols, _, out_width = acc_ref.shape
    n_sel = sel_ref.shape[0]

    @pl.when(step == 0)
    def _():
        acc_ref[...] = jnp.zeros_like(acc_ref)

    rows = x_ref[...]
    gate_proj = jnp.dot(rows, gate_ref[...], preferred_element_type=jnp.float32)
    up_proj = jnp.dot(rows, up_ref[...], preferred_element_type=jnp.float32)
    hidden = (jax.nn.silu(gate_proj) * up_proj).astype(jnp.bfloat16)
    for col in range(n_cols):
        acc_ref[col] += jnp.dot(
            hidden, down_ref[:, col * out_width : (col + 1) * out_width],
            preferred_element_type=jnp.float32,
        )

    @pl.when(step == pl.num_programs(0) - 1)
    def _():
        _, slots, _ = out_ref.shape
        n_groups = n_sel // slots
        for col in range(n_cols):
            picked = jnp.dot(
                sel_ref[...], acc_ref[col], precision=lax.Precision.HIGHEST,
                preferred_element_type=jnp.float32,
            ).astype(out_ref.dtype)
            for slot in range(slots):
                out_ref[col * n_groups : (col + 1) * n_groups, slot, :] = picked[
                    slot * n_groups : (slot + 1) * n_groups
                ]


def expert_ffn(rows, w_gate, w_up, w_down, local, select, n_cols):
    n_rows, width = rows.shape
    n_sel = select.shape[0]
    out_width = width // n_cols
    hidden_units = w_gate.shape[2]
    tile = min(FF_TILE, hidden_units)
    return pl.pallas_call(
        expert_kernel,
        grid=(hidden_units // tile,),
        in_specs=[
            pl.BlockSpec((n_rows, width), lambda f: (0, 0)),
            pl.BlockSpec((None, width, tile), lambda f: (local, 0, f)),
            pl.BlockSpec((None, width, tile), lambda f: (local, 0, f)),
            pl.BlockSpec((None, tile, width), lambda f: (local, f, 0)),
            pl.BlockSpec(select.shape, lambda f: (0, 0)),
        ],
        out_specs=pl.BlockSpec((n_cols * n_sel // CAP, CAP, out_width), lambda f: (0, 0, 0)),
        out_shape=jax.ShapeDtypeStruct((n_cols * n_sel // CAP, CAP, out_width), jnp.bfloat16),
        scratch_shapes=[pltpu.VMEM((n_cols, n_rows, out_width), jnp.float32)],
        compiler_params=pltpu.CompilerParams(vmem_limit_bytes=48 * 1024 * 1024),
    )(rows, w_gate, w_up, w_down, select)


def slot_match(expert_ids, experts, rows_here, n_groups):
    ids = expert_ids.reshape(n_groups, rows_here, expert_ids.shape[1])
    hit = jnp.any(ids[None, :, :, :] == experts[:, None, None, None], axis=-1)
    rank = jnp.cumsum(hit.astype(jnp.int32), axis=-1) - 1
    slot = jnp.arange(CAP, dtype=jnp.int32)
    return hit[:, :, None, :] & (rank[:, :, None, :] == slot[None, None, :, None])


def shards(
    query_rows, key_cache, value_cache, lengths, attn_gain, router, expert_ids, w_gate, w_up, w_down
):
    rows_here = query_rows.shape[0]
    span = key_cache.shape[1]
    kv_share = HEADS // KV_HEADS
    n_grp = lax.axis_size("grp")
    n_shard = lax.axis_size("shard")
    grp_id = lax.axis_index("grp")
    shard_id = lax.axis_index("shard")
    n_blocks = span // BLOCK

    query_heads = query_rows.reshape(rows_here, KV_HEADS, kv_share, HEAD_DIM)
    key_heads = key_cache.reshape(rows_here, span, KV_HEADS, HEAD_DIM)
    value_heads = value_cache.reshape(rows_here, n_blocks, BLOCK, KV_HEADS, HEAD_DIM)
    scores = jnp.einsum(
        "rgjd,rtgd->rgjt", query_heads, key_heads, preferred_element_type=jnp.float32
    ) / math.sqrt(HEAD_DIM)
    position = shard_id * span + jnp.arange(span, dtype=jnp.int32)
    live_mask = (position[None, :] < lengths[:, None])[:, None, None, :]
    scores = jnp.where(live_mask, scores, NEG_FILL)
    scores = scores.reshape(rows_here, KV_HEADS, kv_share, n_blocks, BLOCK)
    live_blocks = live_mask.reshape(rows_here, 1, 1, n_blocks, BLOCK)
    block_max = jnp.max(scores, axis=-1)
    block_probs = jnp.where(live_blocks, jnp.exp(scores - block_max[..., None]), 0.0).astype(
        jnp.bfloat16
    )
    block_sum = jnp.sum(block_probs.astype(jnp.float32), axis=-1)
    block_mix = jnp.einsum(
        "rgjbt,rbtgd->rgjbd", block_probs, value_heads, preferred_element_type=jnp.float32
    )
    dev_max = jnp.max(block_max, axis=-1)
    dev_factor = jnp.exp(block_max - dev_max[..., None])
    dev_sum = jnp.sum(block_sum * dev_factor, axis=-1).reshape(rows_here, HEADS)
    dev_mix = jnp.sum(block_mix * dev_factor[..., None], axis=-2).reshape(rows_here, HEADS, HEAD_DIM)
    dev_max = dev_max.reshape(rows_here, HEADS)

    per_chunk = HEADS // n_shard
    mix_out = dev_mix.reshape(rows_here, n_shard, per_chunk, HEAD_DIM)
    side = jnp.concatenate(
        [dev_max.reshape(rows_here, n_shard, per_chunk), dev_sum.reshape(rows_here, n_shard, per_chunk)],
        axis=-1,
    )
    side = jnp.pad(side, ((0, 0), (0, 0), (0, HEAD_DIM - 2 * per_chunk)))
    packed = jnp.concatenate([mix_out, side[:, :, None, :]], axis=2)
    packed = jnp.transpose(packed, (1, 0, 2, 3))
    stats = lax.all_to_all(packed, "shard", 0, 0, tiled=True)
    got_mix = stats[:, :, :per_chunk, :]
    got_max = stats[:, :, per_chunk, :per_chunk]
    got_sum = stats[:, :, per_chunk, per_chunk : 2 * per_chunk]
    top = jnp.max(got_max, axis=0)
    factor = jnp.exp(got_max - top[None])
    whole_sum = jnp.sum(got_sum * factor, axis=0)
    whole_mix = jnp.sum(got_mix * factor[..., None], axis=0)
    chunk = (whole_mix / whole_sum[..., None]).reshape(rows_here, per_chunk * HEAD_DIM)

    n_dev = n_grp * n_shard
    spread = jnp.broadcast_to(chunk.astype(jnp.bfloat16)[None], (n_dev,) + chunk.shape)
    gathered = lax.all_to_all(spread, ("grp", "shard"), 0, 0, tiled=True).astype(jnp.float32)
    gathered = gathered.reshape(n_grp, n_shard, rows_here, per_chunk * HEAD_DIM)
    attended = jnp.transpose(gathered, (0, 2, 1, 3)).reshape(n_grp * rows_here, -1)

    mean_square = jnp.mean(attended * attended, axis=-1, keepdims=True)
    normed_all = (attended * lax.rsqrt(mean_square + 1e-05) * attn_gain).astype(jnp.bfloat16)
    normed = lax.dynamic_slice_in_dim(normed_all, grp_id * rows_here, rows_here, 0)

    logits = jnp.dot(normed_all, router, preferred_element_type=jnp.float32)
    experts = router.shape[1]
    expert_range = jnp.arange(experts, dtype=jnp.int32)
    expert_hit = expert_ids[:, :, None] == expert_range[None, None, :]
    chosen = jnp.sum(jnp.where(expert_hit, logits[:, None, :], 0.0), axis=-1)
    first_weight = jax.nn.sigmoid(chosen[:, 0] - chosen[:, 1])
    route_weight = jnp.stack([first_weight, 1.0 - first_weight], axis=1)

    local_experts = w_gate.shape[0]
    assert local_experts == 1
    width = normed_all.shape[1]
    out_width = width // n_shard
    expert_index = grp_id
    coefficient = jnp.sum(jnp.where(expert_ids == expert_index, route_weight, 0.0), axis=-1)
    sending = slot_match(expert_ids, expert_index[None], rows_here, n_grp)[0]
    row_of = jnp.arange(n_grp * rows_here, dtype=jnp.int32).reshape(n_grp, 1, rows_here)
    select = jnp.sum(
        jnp.where(
            sending[..., None] & (row_of[..., None] == jnp.arange(n_grp * rows_here)[None, None, None, :]),
            coefficient[None, None, None, :],
            0.0,
        ),
        axis=2,
    )
    select = jnp.transpose(select, (1, 0, 2)).reshape(CAP * n_grp, n_grp * rows_here)
    blocks = expert_ffn(normed_all, w_gate, w_up, w_down, 0, select, n_shard)
    arrived = lax.all_to_all(blocks, ("shard", "grp"), 0, 0, tiled=True)
    arrived = arrived.astype(jnp.float32).reshape(n_shard, n_grp, CAP, out_width)
    per_expert = jnp.sum(arrived, axis=0)
    own_ids = lax.dynamic_slice_in_dim(expert_ids, grp_id * rows_here, rows_here, 0)
    homes = slot_match(own_ids, jnp.arange(n_grp, dtype=jnp.int32) * local_experts, rows_here, 1)[:, 0]
    spread_back = jnp.where(homes[..., None], per_expert[:, :, None, :], 0.0)
    result = jnp.sum(spread_back, axis=(0, 1))
    return (normed, result.astype(jnp.bfloat16))


def solution(mesh):
    in_specs = (
        P("grp", None),
        P("grp", "shard", None),
        P("grp", "shard", None),
        P("grp"),
        P(),
        P(),
        P(),
        P("grp", None, "shard"),
        P("grp", None, "shard"),
        P("grp", "shard", None),
    )
    out_specs = (P("grp", None), P("grp", "shard"))
    return jax.shard_map(shards, mesh=mesh, in_specs=in_specs, out_specs=out_specs, check_vma=False)
```

```python
import math

import jax
import jax.numpy as jnp
from jax import lax
from jax.experimental import pallas as pl
from jax.experimental.pallas import tpu as pltpu
from jax.sharding import PartitionSpec as P

HEADS = 48
KV_HEADS = 8
HEAD_DIM = 128
BLOCK = 256


NEG_FILL = -1e30
CAP = 2


FF_TILE = 512


def expert_kernel(x_ref, gate_ref, up_ref, down_ref, sel_ref, out_ref, acc_ref):
    step = pl.program_id(0)
    n_cols, _, out_width = acc_ref.shape
    n_sel = sel_ref.shape[0]

    @pl.when(step == 0)
    def _():
        acc_ref[...] = jnp.zeros_like(acc_ref)

    rows = x_ref[...]
    gate_proj = jnp.dot(rows, gate_ref[...], preferred_element_type=jnp.float32)
    up_proj = jnp.dot(rows, up_ref[...], preferred_element_type=jnp.float32)
    hidden = (jax.nn.silu(gate_proj) * up_proj).astype(jnp.bfloat16)
    for col in range(n_cols):
        acc_ref[col] += jnp.dot(
            hidden, down_ref[:, col * out_width : (col + 1) * out_width],
            preferred_element_type=jnp.float32,
        )

    @pl.when(step == pl.num_programs(0) - 1)
    def _():
        _, slots, _ = out_ref.shape
        n_groups = n_sel // slots
        for col in range(n_cols):
            picked = jnp.dot(
                sel_ref[...], acc_ref[col], precision=lax.Precision.HIGHEST,
                preferred_element_type=jnp.float32,
            ).astype(out_ref.dtype)
            for slot in range(slots):
                out_ref[col * n_groups : (col + 1) * n_groups, slot, :] = picked[
                    slot * n_groups : (slot + 1) * n_groups
                ]


def expert_ffn(rows, w_gate, w_up, w_down, local, select, n_cols):
    n_rows, width = rows.shape
    n_sel = select.shape[0]
    out_width = width // n_cols
    hidden_units = w_gate.shape[2]
    tile = min(FF_TILE, hidden_units)
    return pl.pallas_call(
        expert_kernel,
        grid=(hidden_units // tile,),
        in_specs=[
            pl.BlockSpec((n_rows, width), lambda f: (0, 0)),
            pl.BlockSpec((None, width, tile), lambda f: (local, 0, f)),
            pl.BlockSpec((None, width, tile), lambda f: (local, 0, f)),
            pl.BlockSpec((None, tile, width), lambda f: (local, f, 0)),
            pl.BlockSpec(select.shape, lambda f: (0, 0)),
        ],
        out_specs=pl.BlockSpec((n_cols * n_sel // CAP, CAP, out_width), lambda f: (0, 0, 0)),
        out_shape=jax.ShapeDtypeStruct((n_cols * n_sel // CAP, CAP, out_width), jnp.bfloat16),
        scratch_shapes=[pltpu.VMEM((n_cols, n_rows, out_width), jnp.float32)],
        compiler_params=pltpu.CompilerParams(vmem_limit_bytes=48 * 1024 * 1024),
    )(rows, w_gate, w_up, w_down, select)


def slot_match(expert_ids, experts, rows_here, n_groups):
    ids = expert_ids.reshape(n_groups, rows_here, expert_ids.shape[1])
    hit = jnp.any(ids[None, :, :, :] == experts[:, None, None, None], axis=-1)
    rank = jnp.cumsum(hit.astype(jnp.int32), axis=-1) - 1
    slot = jnp.arange(CAP, dtype=jnp.int32)
    return hit[:, :, None, :] & (rank[:, :, None, :] == slot[None, None, :, None])


def shards(
    query_rows, key_cache, value_cache, lengths, attn_gain, router, expert_ids, w_gate, w_up, w_down
):
    rows_here = query_rows.shape[0]
    span = key_cache.shape[1]
    kv_share = HEADS // KV_HEADS
    n_grp = lax.axis_size("grp")
    n_shard = lax.axis_size("shard")
    grp_id = lax.axis_index("grp")
    shard_id = lax.axis_index("shard")
    n_blocks = span // BLOCK

    query_heads = query_rows.reshape(rows_here, KV_HEADS, kv_share, HEAD_DIM)
    key_heads = key_cache.reshape(rows_here, span, KV_HEADS, HEAD_DIM)
    value_heads = value_cache.reshape(rows_here, n_blocks, BLOCK, KV_HEADS, HEAD_DIM)
    scores = jnp.einsum(
        "rgjd,rtgd->rgjt", query_heads, key_heads, preferred_element_type=jnp.float32
    ) / math.sqrt(HEAD_DIM)
    position = shard_id * span + jnp.arange(span, dtype=jnp.int32)
    live_mask = (position[None, :] < lengths[:, None])[:, None, None, :]
    scores = jnp.where(live_mask, scores, NEG_FILL)
    scores = scores.reshape(rows_here, KV_HEADS, kv_share, n_blocks, BLOCK)
    live_blocks = live_mask.reshape(rows_here, 1, 1, n_blocks, BLOCK)
    block_max = jnp.max(scores, axis=-1)
    block_probs = jnp.where(live_blocks, jnp.exp(scores - block_max[..., None]), 0.0).astype(
        jnp.bfloat16
    )
    block_sum = jnp.sum(block_probs.astype(jnp.float32), axis=-1)
    block_mix = jnp.einsum(
        "rgjbt,rbtgd->rgjbd", block_probs, value_heads, preferred_element_type=jnp.float32
    )
    dev_max = jnp.max(block_max, axis=-1)
    dev_factor = jnp.exp(block_max - dev_max[..., None])
    dev_sum = jnp.sum(block_sum * dev_factor, axis=-1).reshape(rows_here, HEADS)
    dev_mix = jnp.sum(block_mix * dev_factor[..., None], axis=-2).reshape(rows_here, HEADS, HEAD_DIM)
    dev_max = dev_max.reshape(rows_here, HEADS)

    per_chunk = HEADS // n_shard
    mix_out = dev_mix.reshape(rows_here, n_shard, per_chunk, HEAD_DIM)
    side = jnp.concatenate(
        [dev_max.reshape(rows_here, n_shard, per_chunk), dev_sum.reshape(rows_here, n_shard, per_chunk)],
        axis=-1,
    )
    side = jnp.pad(side, ((0, 0), (0, 0), (0, HEAD_DIM - 2 * per_chunk)))
    packed = jnp.concatenate([mix_out, side[:, :, None, :]], axis=2)
    packed = jnp.transpose(packed, (1, 0, 2, 3))
    stats = lax.all_to_all(packed, "shard", 0, 0, tiled=True)
    got_mix = stats[:, :, :per_chunk, :]
    got_max = stats[:, :, per_chunk, :per_chunk]
    got_sum = stats[:, :, per_chunk, per_chunk : 2 * per_chunk]
    top = jnp.max(got_max, axis=0)
    factor = jnp.exp(got_max - top[None])
    whole_sum = jnp.sum(got_sum * factor, axis=0)
    whole_mix = jnp.sum(got_mix * factor[..., None], axis=0)
    chunk = (whole_mix / whole_sum[..., None]).reshape(rows_here, per_chunk * HEAD_DIM)

    n_dev = n_grp * n_shard
    spread = jnp.broadcast_to(chunk.astype(jnp.bfloat16)[None], (n_dev,) + chunk.shape)
    gathered = lax.all_to_all(spread, ("grp", "shard"), 0, 0, tiled=True).astype(jnp.float32)
    gathered = gathered.reshape(n_grp, n_shard, rows_here, per_chunk * HEAD_DIM)
    attended = jnp.transpose(gathered, (0, 2, 1, 3)).reshape(n_grp * rows_here, -1)

    mean_square = jnp.mean(attended * attended, axis=-1, keepdims=True)
    normed_all = (attended * lax.rsqrt(mean_square + 1e-05) * attn_gain).astype(jnp.bfloat16)
    normed = lax.dynamic_slice_in_dim(normed_all, grp_id * rows_here, rows_here, 0)

    logits = jnp.dot(normed_all, router, preferred_element_type=jnp.float32)
    experts = router.shape[1]
    expert_range = jnp.arange(experts, dtype=jnp.int32)
    expert_hit = expert_ids[:, :, None] == expert_range[None, None, :]
    chosen = jnp.sum(jnp.where(expert_hit, logits[:, None, :], 0.0), axis=-1)
    first_weight = jax.nn.sigmoid(chosen[:, 0] - chosen[:, 1])
    route_weight = jnp.stack([first_weight, 1.0 - first_weight], axis=1)

    local_experts = w_gate.shape[0]
    assert local_experts == 1
    width = normed_all.shape[1]
    out_width = width // n_shard
    expert_index = grp_id
    coefficient = jnp.sum(jnp.where(expert_ids == expert_index, route_weight, 0.0), axis=-1)
    sending = slot_match(expert_ids, expert_index[None], rows_here, n_grp)[0]
    row_of = jnp.arange(n_grp * rows_here, dtype=jnp.int32).reshape(n_grp, 1, rows_here)
    select = jnp.sum(
        jnp.where(
            sending[..., None] & (row_of[..., None] == jnp.arange(n_grp * rows_here)[None, None, None, :]),
            coefficient[None, None, None, :],
            0.0,
        ),
        axis=2,
    )
    select = jnp.transpose(select, (1, 0, 2)).reshape(CAP * n_grp, n_grp * rows_here)
    blocks = expert_ffn(normed_all, w_gate, w_up, w_down, 0, select, n_shard)
    arrived = lax.all_to_all(blocks, ("shard", "grp"), 0, 0, tiled=True)
    arrived = arrived.astype(jnp.float32).reshape(n_shard, n_grp, CAP, out_width)
    per_expert = jnp.sum(arrived, axis=0)
    own_ids = lax.dynamic_slice_in_dim(expert_ids, grp_id * rows_here, rows_here, 0)
    homes = slot_match(own_ids, jnp.arange(n_grp, dtype=jnp.int32) * local_experts, rows_here, 1)[:, 0]
    spread_back = jnp.where(homes[..., None], per_expert[:, :, None, :], 0.0)
    result = jnp.sum(spread_back, axis=(0, 1))
    return (normed, result.astype(jnp.bfloat16))


def solution(mesh):
    in_specs = (
        P("grp", None),
        P("grp", "shard", None),
        P("grp", "shard", None),
        P("grp"),
        P(),
        P(),
        P(),
        P("grp", None, "shard"),
        P("grp", None, "shard"),
        P("grp", "shard", None),
    )
    out_specs = (P("grp", None), P("grp", "shard"))
    return jax.shard_map(shards, mesh=mesh, in_specs=in_specs, out_specs=out_specs, check_vma=False)
```

```python
import math

import jax
import jax.numpy as jnp
from jax import lax
from jax.experimental import pallas as pl
from jax.experimental.pallas import tpu as pltpu
from jax.sharding import PartitionSpec as P

HEADS = 48
KV_HEADS = 8
HEAD_DIM = 128
BLOCK = 256


NEG_FILL = -1e30
CAP = 2


FF_TILE = 128


def expert_kernel(x_ref, gate_ref, up_ref, down_ref, sel_ref, out_ref, acc_ref):
    step = pl.program_id(0)
    n_cols, _, out_width = acc_ref.shape
    n_sel = sel_ref.shape[0]

    @pl.when(step == 0)
    def _():
        acc_ref[...] = jnp.zeros_like(acc_ref)

    rows = x_ref[...]
    gate_proj = jnp.dot(rows, gate_ref[...], preferred_element_type=jnp.float32)
    up_proj = jnp.dot(rows, up_ref[...], preferred_element_type=jnp.float32)
    hidden = (jax.nn.silu(gate_proj) * up_proj).astype(jnp.bfloat16)
    for col in range(n_cols):
        acc_ref[col] += jnp.dot(
            hidden, down_ref[:, col * out_width : (col + 1) * out_width],
            preferred_element_type=jnp.float32,
        )

    @pl.when(step == pl.num_programs(0) - 1)
    def _():
        _, slots, _ = out_ref.shape
        n_groups = n_sel // slots
        for col in range(n_cols):
            picked = jnp.dot(
                sel_ref[...], acc_ref[col], precision=lax.Precision.HIGHEST,
                preferred_element_type=jnp.float32,
            ).astype(out_ref.dtype)
            for slot in range(slots):
                out_ref[col * n_groups : (col + 1) * n_groups, slot, :] = picked[
                    slot * n_groups : (slot + 1) * n_groups
                ]


def expert_ffn(rows, w_gate, w_up, w_down, local, select, n_cols):
    n_rows, width = rows.shape
    n_sel = select.shape[0]
    out_width = width // n_cols
    hidden_units = w_gate.shape[2]
    tile = min(FF_TILE, hidden_units)
    return pl.pallas_call(
        expert_kernel,
        grid=(hidden_units // tile,),
        in_specs=[
            pl.BlockSpec((n_rows, width), lambda f: (0, 0)),
            pl.BlockSpec((None, width, tile), lambda f: (local, 0, f)),
            pl.BlockSpec((None, width, tile), lambda f: (local, 0, f)),
            pl.BlockSpec((None, tile, width), lambda f: (local, f, 0)),
            pl.BlockSpec(select.shape, lambda f: (0, 0)),
        ],
        out_specs=pl.BlockSpec((n_cols * n_sel // CAP, CAP, out_width), lambda f: (0, 0, 0)),
        out_shape=jax.ShapeDtypeStruct((n_cols * n_sel // CAP, CAP, out_width), jnp.bfloat16),
        scratch_shapes=[pltpu.VMEM((n_cols, n_rows, out_width), jnp.float32)],
        compiler_params=pltpu.CompilerParams(vmem_limit_bytes=48 * 1024 * 1024),
    )(rows, w_gate, w_up, w_down, select)


def slot_match(expert_ids, experts, rows_here, n_groups):
    ids = expert_ids.reshape(n_groups, rows_here, expert_ids.shape[1])
    hit = jnp.any(ids[None, :, :, :] == experts[:, None, None, None], axis=-1)
    rank = jnp.cumsum(hit.astype(jnp.int32), axis=-1) - 1
    slot = jnp.arange(CAP, dtype=jnp.int32)
    return hit[:, :, None, :] & (rank[:, :, None, :] == slot[None, None, :, None])


def shards(
    query_rows, key_cache, value_cache, lengths, attn_gain, router, expert_ids, w_gate, w_up, w_down
):
    rows_here = query_rows.shape[0]
    span = key_cache.shape[1]
    kv_share = HEADS // KV_HEADS
    n_grp = lax.axis_size("grp")
    n_shard = lax.axis_size("shard")
    grp_id = lax.axis_index("grp")
    shard_id = lax.axis_index("shard")
    n_blocks = span // BLOCK

    query_heads = query_rows.reshape(rows_here, KV_HEADS, kv_share, HEAD_DIM)
    key_heads = key_cache.reshape(rows_here, span, KV_HEADS, HEAD_DIM)
    value_heads = value_cache.reshape(rows_here, n_blocks, BLOCK, KV_HEADS, HEAD_DIM)
    scores = jnp.einsum(
        "rgjd,rtgd->rgjt", query_heads, key_heads, preferred_element_type=jnp.float32
    ) / math.sqrt(HEAD_DIM)
    position = shard_id * span + jnp.arange(span, dtype=jnp.int32)
    live_mask = (position[None, :] < lengths[:, None])[:, None, None, :]
    scores = jnp.where(live_mask, scores, NEG_FILL)
    scores = scores.reshape(rows_here, KV_HEADS, kv_share, n_blocks, BLOCK)
    live_blocks = live_mask.reshape(rows_here, 1, 1, n_blocks, BLOCK)
    block_max = jnp.max(scores, axis=-1)
    block_probs = jnp.where(live_blocks, jnp.exp(scores - block_max[..., None]), 0.0).astype(
        jnp.bfloat16
    )
    block_sum = jnp.sum(block_probs.astype(jnp.float32), axis=-1)
    block_mix = jnp.einsum(
        "rgjbt,rbtgd->rgjbd", block_probs, value_heads, preferred_element_type=jnp.float32
    )
    dev_max = jnp.max(block_max, axis=-1)
    dev_factor = jnp.exp(block_max - dev_max[..., None])
    dev_sum = jnp.sum(block_sum * dev_factor, axis=-1).reshape(rows_here, HEADS)
    dev_mix = jnp.sum(block_mix * dev_factor[..., None], axis=-2).reshape(rows_here, HEADS, HEAD_DIM)
    dev_max = dev_max.reshape(rows_here, HEADS)

    per_chunk = HEADS // n_shard
    mix_out = dev_mix.reshape(rows_here, n_shard, per_chunk, HEAD_DIM)
    side = jnp.concatenate(
        [dev_max.reshape(rows_here, n_shard, per_chunk), dev_sum.reshape(rows_here, n_shard, per_chunk)],
        axis=-1,
    )
    side = jnp.pad(side, ((0, 0), (0, 0), (0, HEAD_DIM - 2 * per_chunk)))
    packed = jnp.concatenate([mix_out, side[:, :, None, :]], axis=2)
    packed = jnp.transpose(packed, (1, 0, 2, 3))
    stats = lax.all_to_all(packed, "shard", 0, 0, tiled=True)
    got_mix = stats[:, :, :per_chunk, :]
    got_max = stats[:, :, per_chunk, :per_chunk]
    got_sum = stats[:, :, per_chunk, per_chunk : 2 * per_chunk]
    top = jnp.max(got_max, axis=0)
    factor = jnp.exp(got_max - top[None])
    whole_sum = jnp.sum(got_sum * factor, axis=0)
    whole_mix = jnp.sum(got_mix * factor[..., None], axis=0)
    chunk = (whole_mix / whole_sum[..., None]).reshape(rows_here, per_chunk * HEAD_DIM)

    n_dev = n_grp * n_shard
    spread = jnp.broadcast_to(chunk.astype(jnp.bfloat16)[None], (n_dev,) + chunk.shape)
    gathered = lax.all_to_all(spread, ("grp", "shard"), 0, 0, tiled=True).astype(jnp.float32)
    gathered = gathered.reshape(n_grp, n_shard, rows_here, per_chunk * HEAD_DIM)
    attended = jnp.transpose(gathered, (0, 2, 1, 3)).reshape(n_grp * rows_here, -1)

    mean_square = jnp.mean(attended * attended, axis=-1, keepdims=True)
    normed_all = (attended * lax.rsqrt(mean_square + 1e-05) * attn_gain).astype(jnp.bfloat16)
    normed = lax.dynamic_slice_in_dim(normed_all, grp_id * rows_here, rows_here, 0)

    logits = jnp.dot(normed_all, router, preferred_element_type=jnp.float32)
    experts = router.shape[1]
    expert_range = jnp.arange(experts, dtype=jnp.int32)
    expert_hit = expert_ids[:, :, None] == expert_range[None, None, :]
    chosen = jnp.sum(jnp.where(expert_hit, logits[:, None, :], 0.0), axis=-1)
    first_weight = jax.nn.sigmoid(chosen[:, 0] - chosen[:, 1])
    route_weight = jnp.stack([first_weight, 1.0 - first_weight], axis=1)

    local_experts = w_gate.shape[0]
    assert local_experts == 1
    width = normed_all.shape[1]
    out_width = width // n_shard
    expert_index = grp_id
    coefficient = jnp.sum(jnp.where(expert_ids == expert_index, route_weight, 0.0), axis=-1)
    sending = slot_match(expert_ids, expert_index[None], rows_here, n_grp)[0]
    row_of = jnp.arange(n_grp * rows_here, dtype=jnp.int32).reshape(n_grp, 1, rows_here)
    select = jnp.sum(
        jnp.where(
            sending[..., None] & (row_of[..., None] == jnp.arange(n_grp * rows_here)[None, None, None, :]),
            coefficient[None, None, None, :],
            0.0,
        ),
        axis=2,
    )
    select = jnp.transpose(select, (1, 0, 2)).reshape(CAP * n_grp, n_grp * rows_here)
    blocks = expert_ffn(normed_all, w_gate, w_up, w_down, 0, select, n_shard)
    arrived = lax.all_to_all(blocks, ("shard", "grp"), 0, 0, tiled=True)
    arrived = arrived.astype(jnp.float32).reshape(n_shard, n_grp, CAP, out_width)
    per_expert = jnp.sum(arrived, axis=0)
    own_ids = lax.dynamic_slice_in_dim(expert_ids, grp_id * rows_here, rows_here, 0)
    homes = slot_match(own_ids, jnp.arange(n_grp, dtype=jnp.int32) * local_experts, rows_here, 1)[:, 0]
    spread_back = jnp.where(homes[..., None], per_expert[:, :, None, :], 0.0)
    result = jnp.sum(spread_back, axis=(0, 1))
    return (normed, result.astype(jnp.bfloat16))


def solution(mesh):
    in_specs = (
        P("grp", None),
        P("grp", "shard", None),
        P("grp", "shard", None),
        P("grp"),
        P(),
        P(),
        P(),
        P("grp", None, "shard"),
        P("grp", None, "shard"),
        P("grp", "shard", None),
    )
    out_specs = (P("grp", None), P("grp", "shard"))
    return jax.shard_map(shards, mesh=mesh, in_specs=in_specs, out_specs=out_specs, check_vma=False)
```

```python
import math

import jax
import jax.numpy as jnp
from jax import lax
from jax.experimental import pallas as pl
from jax.experimental.pallas import tpu as pltpu
from jax.sharding import PartitionSpec as P

HEADS = 48
KV_HEADS = 8
HEAD_DIM = 128
BLOCK = 256


NEG_FILL = -1e30
CAP = 2


FF_TILE = 256


def expert_kernel(x_ref, gate_ref, up_ref, down_ref, sel_ref, out_ref, acc_ref):
    step = pl.program_id(0)

    @pl.when(step == 0)
    def _():
        acc_ref[...] = jnp.zeros_like(acc_ref)

    rows = x_ref[...]
    gate_proj = jnp.dot(rows, gate_ref[...], preferred_element_type=jnp.float32)
    up_proj = jnp.dot(rows, up_ref[...], preferred_element_type=jnp.float32)
    hidden = (jax.nn.silu(gate_proj) * up_proj).astype(jnp.bfloat16)
    acc_ref[...] += jnp.dot(hidden, down_ref[...], preferred_element_type=jnp.float32)

    @pl.when(step == pl.num_programs(0) - 1)
    def _():
        picked = jnp.dot(
            sel_ref[...], acc_ref[...], precision=lax.Precision.HIGHEST,
            preferred_element_type=jnp.float32,
        )
        out_ref[...] = picked.astype(out_ref.dtype)


def expert_ffn(rows, w_gate, w_up, w_down, local, select):
    n_rows, width = rows.shape
    n_out = select.shape[0]
    hidden_units = w_gate.shape[2]
    tile = min(FF_TILE, hidden_units)
    return pl.pallas_call(
        expert_kernel,
        grid=(hidden_units // tile,),
        in_specs=[
            pl.BlockSpec((n_rows, width), lambda f: (0, 0)),
            pl.BlockSpec((None, width, tile), lambda f: (local, 0, f)),
            pl.BlockSpec((None, width, tile), lambda f: (local, 0, f)),
            pl.BlockSpec((None, tile, width), lambda f: (local, f, 0)),
            pl.BlockSpec((n_out, n_rows), lambda f: (0, 0)),
        ],
        out_specs=pl.BlockSpec((n_out, width), lambda f: (0, 0)),
        out_shape=jax.ShapeDtypeStruct((n_out, width), jnp.float32),
        scratch_shapes=[pltpu.VMEM((n_rows, width), jnp.float32)],
        compiler_params=pltpu.CompilerParams(vmem_limit_bytes=48 * 1024 * 1024),
    )(rows, w_gate, w_up, w_down, select)


def slot_match(expert_ids, experts, rows_here, n_groups):
    ids = expert_ids.reshape(n_groups, rows_here, expert_ids.shape[1])
    hit = jnp.any(ids[None, :, :, :] == experts[:, None, None, None], axis=-1)
    rank = jnp.cumsum(hit.astype(jnp.int32), axis=-1) - 1
    slot = jnp.arange(CAP, dtype=jnp.int32)
    return hit[:, :, None, :] & (rank[:, :, None, :] == slot[None, None, :, None])


def shards(
    query_rows, key_cache, value_cache, lengths, attn_gain, router, expert_ids, w_gate, w_up, w_down
):
    rows_here = query_rows.shape[0]
    span = key_cache.shape[1]
    kv_share = HEADS // KV_HEADS
    n_grp = lax.axis_size("grp")
    n_shard = lax.axis_size("shard")
    grp_id = lax.axis_index("grp")
    shard_id = lax.axis_index("shard")
    n_blocks = span // BLOCK

    query_heads = query_rows.reshape(rows_here, KV_HEADS, kv_share, HEAD_DIM)
    key_heads = key_cache.reshape(rows_here, span, KV_HEADS, HEAD_DIM)
    value_heads = value_cache.reshape(rows_here, n_blocks, BLOCK, KV_HEADS, HEAD_DIM)
    scores = jnp.einsum(
        "rgjd,rtgd->rgjt", query_heads, key_heads, preferred_element_type=jnp.float32
    ) / math.sqrt(HEAD_DIM)
    position = shard_id * span + jnp.arange(span, dtype=jnp.int32)
    live_mask = (position[None, :] < lengths[:, None])[:, None, None, :]
    scores = jnp.where(live_mask, scores, NEG_FILL)
    scores = scores.reshape(rows_here, KV_HEADS, kv_share, n_blocks, BLOCK)
    live_blocks = live_mask.reshape(rows_here, 1, 1, n_blocks, BLOCK)
    block_max = jnp.max(scores, axis=-1)
    block_probs = jnp.where(live_blocks, jnp.exp(scores - block_max[..., None]), 0.0).astype(
        jnp.bfloat16
    )
    block_sum = jnp.sum(block_probs.astype(jnp.float32), axis=-1)
    block_mix = jnp.einsum(
        "rgjbt,rbtgd->rgjbd", block_probs, value_heads, preferred_element_type=jnp.float32
    )
    dev_max = jnp.max(block_max, axis=-1)
    dev_factor = jnp.exp(block_max - dev_max[..., None])
    dev_sum = jnp.sum(block_sum * dev_factor, axis=-1).reshape(rows_here, HEADS)
    dev_mix = jnp.sum(block_mix * dev_factor[..., None], axis=-2).reshape(rows_here, HEADS, HEAD_DIM)
    dev_max = dev_max.reshape(rows_here, HEADS)

    per_chunk = HEADS // n_shard
    mix_out = dev_mix.reshape(rows_here, n_shard, per_chunk, HEAD_DIM)
    side = jnp.concatenate(
        [dev_max.reshape(rows_here, n_shard, per_chunk), dev_sum.reshape(rows_here, n_shard, per_chunk)],
        axis=-1,
    )
    side = jnp.pad(side, ((0, 0), (0, 0), (0, HEAD_DIM - 2 * per_chunk)))
    packed = jnp.concatenate([mix_out, side[:, :, None, :]], axis=2)
    packed = jnp.transpose(packed, (1, 0, 2, 3))
    stats = lax.all_to_all(packed, "shard", 0, 0, tiled=True)
    got_mix = stats[:, :, :per_chunk, :]
    got_max = stats[:, :, per_chunk, :per_chunk]
    got_sum = stats[:, :, per_chunk, per_chunk : 2 * per_chunk]
    top = jnp.max(got_max, axis=0)
    factor = jnp.exp(got_max - top[None])
    whole_sum = jnp.sum(got_sum * factor, axis=0)
    whole_mix = jnp.sum(got_mix * factor[..., None], axis=0)
    chunk = (whole_mix / whole_sum[..., None]).reshape(rows_here, per_chunk * HEAD_DIM)

    n_dev = n_grp * n_shard
    spread = jnp.broadcast_to(chunk.astype(jnp.bfloat16)[None], (n_dev,) + chunk.shape)
    gathered = lax.all_to_all(spread, ("grp", "shard"), 0, 0, tiled=True).astype(jnp.float32)
    gathered = gathered.reshape(n_grp, n_shard, rows_here, per_chunk * HEAD_DIM)
    attended = jnp.transpose(gathered, (0, 2, 1, 3)).reshape(n_grp * rows_here, -1)

    mean_square = jnp.mean(attended * attended, axis=-1, keepdims=True)
    normed_all = (attended * lax.rsqrt(mean_square + 1e-05) * attn_gain).astype(jnp.bfloat16)
    normed = lax.dynamic_slice_in_dim(normed_all, grp_id * rows_here, rows_here, 0)

    logits = jnp.dot(normed_all, router, preferred_element_type=jnp.float32)
    experts = router.shape[1]
    expert_range = jnp.arange(experts, dtype=jnp.int32)
    expert_hit = expert_ids[:, :, None] == expert_range[None, None, :]
    chosen = jnp.sum(jnp.where(expert_hit, logits[:, None, :], 0.0), axis=-1)
    first_weight = jax.nn.sigmoid(chosen[:, 0] - chosen[:, 1])
    route_weight = jnp.stack([first_weight, 1.0 - first_weight], axis=1)

    local_experts = w_gate.shape[0]
    assert local_experts == 1
    width = normed_all.shape[1]
    out_width = width // n_shard
    expert_index = grp_id
    coefficient = jnp.sum(jnp.where(expert_ids == expert_index, route_weight, 0.0), axis=-1)
    sending = slot_match(expert_ids, expert_index[None], rows_here, n_grp)[0]
    row_of = jnp.arange(n_grp * rows_here, dtype=jnp.int32).reshape(n_grp, 1, rows_here)
    select = jnp.sum(
        jnp.where(
            sending[..., None] & (row_of[..., None] == jnp.arange(n_grp * rows_here)[None, None, None, :]),
            coefficient[None, None, None, :],
            0.0,
        ),
        axis=2,
    )
    select = jnp.transpose(select, (1, 0, 2)).reshape(CAP * n_grp, n_grp * rows_here)
    picked = expert_ffn(normed_all, w_gate, w_up, w_down, 0, select)
    blocks = picked.reshape(CAP, n_dev, out_width)
    arrived = lax.all_to_all(blocks, ("grp", "shard"), 1, 1, tiled=True)
    arrived = arrived.reshape(CAP, n_grp, n_shard, out_width)
    per_expert = jnp.transpose(jnp.sum(arrived, axis=2), (1, 0, 2))
    own_ids = lax.dynamic_slice_in_dim(expert_ids, grp_id * rows_here, rows_here, 0)
    homes = slot_match(own_ids, jnp.arange(n_grp, dtype=jnp.int32) * local_experts, rows_here, 1)[:, 0]
    spread_back = jnp.where(homes[..., None], per_expert[:, :, None, :], 0.0)
    result = jnp.sum(spread_back, axis=(0, 1))
    return (normed, result.astype(jnp.bfloat16))


def solution(mesh):
    in_specs = (
        P("grp", None),
        P("grp", "shard", None),
        P("grp", "shard", None),
        P("grp"),
        P(),
        P(),
        P(),
        P("grp", None, "shard"),
        P("grp", None, "shard"),
        P("grp", "shard", None),
    )
    out_specs = (P("grp", None), P("grp", "shard"))
    return jax.shard_map(shards, mesh=mesh, in_specs=in_specs, out_specs=out_specs, check_vma=False)
```

```python
import math

import jax
import jax.numpy as jnp
from jax import lax
from jax.experimental import pallas as pl
from jax.experimental.pallas import tpu as pltpu
from jax.sharding import PartitionSpec as P

HEADS = 48
KV_HEADS = 8
HEAD_DIM = 128
BLOCK = 256


NEG_FILL = -1e30
CAP = 2


FF_TILE = 256


def expert_kernel(x_ref, gate_ref, up_ref, down_ref, sel_ref, out_ref, acc_ref):
    step = pl.program_id(0)
    n_cols, _, out_width = acc_ref.shape
    n_sel = sel_ref.shape[0]

    @pl.when(step == 0)
    def _():
        acc_ref[...] = jnp.zeros_like(acc_ref)

    rows = x_ref[...]
    gate_proj = jnp.dot(rows, gate_ref[...], preferred_element_type=jnp.float32)
    up_proj = jnp.dot(rows, up_ref[...], preferred_element_type=jnp.float32)
    hidden = (jax.nn.silu(gate_proj) * up_proj).astype(jnp.bfloat16)
    for col in range(n_cols):
        acc_ref[col] += jnp.dot(
            hidden, down_ref[:, col * out_width : (col + 1) * out_width],
            preferred_element_type=jnp.float32,
        )

    @pl.when(step == pl.num_programs(0) - 1)
    def _():
        _, slots, _ = out_ref.shape
        n_groups = n_sel // slots
        for col in range(n_cols):
            picked = jnp.dot(
                sel_ref[...], acc_ref[col], precision=lax.Precision.HIGHEST,
                preferred_element_type=jnp.float32,
            ).astype(out_ref.dtype)
            for slot in range(slots):
                out_ref[col * n_groups : (col + 1) * n_groups, slot, :] = picked[
                    slot * n_groups : (slot + 1) * n_groups
                ]


def expert_ffn(rows, w_gate, w_up, w_down, local, select, n_cols):
    n_rows, width = rows.shape
    n_sel = select.shape[0]
    out_width = width // n_cols
    hidden_units = w_gate.shape[2]
    tile = min(FF_TILE, hidden_units)
    return pl.pallas_call(
        expert_kernel,
        grid=(hidden_units // tile,),
        in_specs=[
            pl.BlockSpec((n_rows, width), lambda f: (0, 0)),
            pl.BlockSpec((None, width, tile), lambda f: (local, 0, f)),
            pl.BlockSpec((None, width, tile), lambda f: (local, 0, f)),
            pl.BlockSpec((None, tile, width), lambda f: (local, f, 0)),
            pl.BlockSpec(select.shape, lambda f: (0, 0)),
        ],
        out_specs=pl.BlockSpec((n_cols * n_sel // CAP, CAP, out_width), lambda f: (0, 0, 0)),
        out_shape=jax.ShapeDtypeStruct((n_cols * n_sel // CAP, CAP, out_width), jnp.float32),
        scratch_shapes=[pltpu.VMEM((n_cols, n_rows, out_width), jnp.float32)],
        compiler_params=pltpu.CompilerParams(vmem_limit_bytes=48 * 1024 * 1024),
    )(rows, w_gate, w_up, w_down, select)


def slot_match(expert_ids, experts, rows_here, n_groups):
    ids = expert_ids.reshape(n_groups, rows_here, expert_ids.shape[1])
    hit = jnp.any(ids[None, :, :, :] == experts[:, None, None, None], axis=-1)
    rank = jnp.cumsum(hit.astype(jnp.int32), axis=-1) - 1
    slot = jnp.arange(CAP, dtype=jnp.int32)
    return hit[:, :, None, :] & (rank[:, :, None, :] == slot[None, None, :, None])


def shards(
    query_rows, key_cache, value_cache, lengths, attn_gain, router, expert_ids, w_gate, w_up, w_down
):
    rows_here = query_rows.shape[0]
    span = key_cache.shape[1]
    kv_share = HEADS // KV_HEADS
    n_grp = lax.axis_size("grp")
    n_shard = lax.axis_size("shard")
    grp_id = lax.axis_index("grp")
    shard_id = lax.axis_index("shard")
    n_blocks = span // BLOCK

    query_heads = query_rows.reshape(rows_here, KV_HEADS, kv_share, HEAD_DIM)
    key_heads = key_cache.reshape(rows_here, span, KV_HEADS, HEAD_DIM)
    value_heads = value_cache.reshape(rows_here, n_blocks, BLOCK, KV_HEADS, HEAD_DIM)
    scores = jnp.einsum(
        "rgjd,rtgd->rgjt", query_heads, key_heads, preferred_element_type=jnp.float32
    ) / math.sqrt(HEAD_DIM)
    position = shard_id * span + jnp.arange(span, dtype=jnp.int32)
    live_mask = (position[None, :] < lengths[:, None])[:, None, None, :]
    scores = jnp.where(live_mask, scores, NEG_FILL)
    scores = scores.reshape(rows_here, KV_HEADS, kv_share, n_blocks, BLOCK)
    live_blocks = live_mask.reshape(rows_here, 1, 1, n_blocks, BLOCK)
    block_max = jnp.max(scores, axis=-1)
    block_probs = jnp.where(live_blocks, jnp.exp(scores - block_max[..., None]), 0.0).astype(
        jnp.bfloat16
    )
    block_sum = jnp.sum(block_probs.astype(jnp.float32), axis=-1)
    block_mix = jnp.einsum(
        "rgjbt,rbtgd->rgjbd", block_probs, value_heads, preferred_element_type=jnp.float32
    )
    dev_max = jnp.max(block_max, axis=-1)
    dev_factor = jnp.exp(block_max - dev_max[..., None])
    dev_sum = jnp.sum(block_sum * dev_factor, axis=-1).reshape(rows_here, HEADS)
    dev_mix = jnp.sum(block_mix * dev_factor[..., None], axis=-2).reshape(rows_here, HEADS, HEAD_DIM)
    dev_max = dev_max.reshape(rows_here, HEADS)

    per_chunk = HEADS // n_shard
    mix_out = dev_mix.reshape(rows_here, n_shard, per_chunk, HEAD_DIM)
    side = jnp.concatenate(
        [dev_max.reshape(rows_here, n_shard, per_chunk), dev_sum.reshape(rows_here, n_shard, per_chunk)],
        axis=-1,
    )
    side = jnp.pad(side, ((0, 0), (0, 0), (0, HEAD_DIM - 2 * per_chunk)))
    packed = jnp.concatenate([mix_out, side[:, :, None, :]], axis=2)
    packed = jnp.transpose(packed, (1, 0, 2, 3))
    stats = lax.all_to_all(packed, "shard", 0, 0, tiled=True)
    got_mix = stats[:, :, :per_chunk, :]
    got_max = stats[:, :, per_chunk, :per_chunk]
    got_sum = stats[:, :, per_chunk, per_chunk : 2 * per_chunk]
    top = jnp.max(got_max, axis=0)
    factor = jnp.exp(got_max - top[None])
    whole_sum = jnp.sum(got_sum * factor, axis=0)
    whole_mix = jnp.sum(got_mix * factor[..., None], axis=0)
    chunk = (whole_mix / whole_sum[..., None]).reshape(rows_here, per_chunk * HEAD_DIM)

    n_dev = n_grp * n_shard
    spread = jnp.broadcast_to(chunk.astype(jnp.bfloat16)[None], (n_dev,) + chunk.shape)
    gathered = lax.all_to_all(spread, ("grp", "shard"), 0, 0, tiled=True).astype(jnp.float32)
    gathered = gathered.reshape(n_grp, n_shard, rows_here, per_chunk * HEAD_DIM)
    attended = jnp.transpose(gathered, (0, 2, 1, 3)).reshape(n_grp * rows_here, -1)

    mean_square = jnp.mean(attended * attended, axis=-1, keepdims=True)
    normed_all = (attended * lax.rsqrt(mean_square + 1e-05) * attn_gain).astype(jnp.bfloat16)
    normed = lax.dynamic_slice_in_dim(normed_all, grp_id * rows_here, rows_here, 0)

    logits = jnp.dot(normed_all, router, preferred_element_type=jnp.float32)
    experts = router.shape[1]
    expert_range = jnp.arange(experts, dtype=jnp.int32)
    expert_hit = expert_ids[:, :, None] == expert_range[None, None, :]
    chosen = jnp.sum(jnp.where(expert_hit, logits[:, None, :], 0.0), axis=-1)
    first_weight = jax.nn.sigmoid(chosen[:, 0] - chosen[:, 1])
    route_weight = jnp.stack([first_weight, 1.0 - first_weight], axis=1)

    local_experts = w_gate.shape[0]
    assert local_experts == 1
    width = normed_all.shape[1]
    out_width = width // n_shard
    expert_index = grp_id
    coefficient = jnp.sum(jnp.where(expert_ids == expert_index, route_weight, 0.0), axis=-1)
    sending = slot_match(expert_ids, expert_index[None], rows_here, n_grp)[0]
    row_of = jnp.arange(n_grp * rows_here, dtype=jnp.int32).reshape(n_grp, 1, rows_here)
    select = jnp.sum(
        jnp.where(
            sending[..., None] & (row_of[..., None] == jnp.arange(n_grp * rows_here)[None, None, None, :]),
            coefficient[None, None, None, :],
            0.0,
        ),
        axis=2,
    )
    select = jnp.transpose(select, (1, 0, 2)).reshape(CAP * n_grp, n_grp * rows_here)
    blocks = expert_ffn(normed_all, w_gate, w_up, w_down, 0, select, n_shard)
    arrived = lax.all_to_all(blocks, ("shard", "grp"), 0, 0, tiled=True)
    arrived = arrived.reshape(n_shard, n_grp, CAP, out_width)
    per_expert = jnp.sum(arrived, axis=0)
    own_ids = lax.dynamic_slice_in_dim(expert_ids, grp_id * rows_here, rows_here, 0)
    homes = slot_match(own_ids, jnp.arange(n_grp, dtype=jnp.int32) * local_experts, rows_here, 1)[:, 0]
    spread_back = jnp.where(homes[..., None], per_expert[:, :, None, :], 0.0)
    result = jnp.sum(spread_back, axis=(0, 1))
    return (normed, result.astype(jnp.bfloat16))


def solution(mesh):
    in_specs = (
        P("grp", None),
        P("grp", "shard", None),
        P("grp", "shard", None),
        P("grp"),
        P(),
        P(),
        P(),
        P("grp", None, "shard"),
        P("grp", None, "shard"),
        P("grp", "shard", None),
    )
    out_specs = (P("grp", None), P("grp", "shard"))
    return jax.shard_map(shards, mesh=mesh, in_specs=in_specs, out_specs=out_specs, check_vma=False)
```

```python
import math

import jax
import jax.numpy as jnp
from jax import lax
from jax.experimental import pallas as pl
from jax.experimental.pallas import tpu as pltpu
from jax.sharding import PartitionSpec as P

HEADS = 48
KV_HEADS = 8
HEAD_DIM = 128
BLOCK = 256


NEG_FILL = -1e30
CAP = 2


FF_TILE = 256


def expert_kernel(x_ref, gate_ref, up_ref, down_ref, sel_ref, out_ref, acc_ref):
    step = pl.program_id(0)

    @pl.when(step == 0)
    def _():
        acc_ref[...] = jnp.zeros_like(acc_ref)

    rows = x_ref[...]
    gate_proj = jnp.dot(rows, gate_ref[...], preferred_element_type=jnp.float32)
    up_proj = jnp.dot(rows, up_ref[...], preferred_element_type=jnp.float32)
    hidden = (jax.nn.silu(gate_proj) * up_proj).astype(jnp.bfloat16)
    acc_ref[...] += jnp.dot(hidden, down_ref[...], preferred_element_type=jnp.float32)

    @pl.when(step == pl.num_programs(0) - 1)
    def _():
        picked = jnp.dot(
            sel_ref[...], acc_ref[...], precision=lax.Precision.HIGHEST,
            preferred_element_type=jnp.float32,
        )
        out_ref[...] = picked.astype(out_ref.dtype)


def expert_ffn(rows, w_gate, w_up, w_down, local, select):
    n_rows, width = rows.shape
    n_out = select.shape[0]
    hidden_units = w_gate.shape[2]
    tile = min(FF_TILE, hidden_units)
    return pl.pallas_call(
        expert_kernel,
        grid=(hidden_units // tile,),
        in_specs=[
            pl.BlockSpec((n_rows, width), lambda f: (0, 0)),
            pl.BlockSpec((None, width, tile), lambda f: (local, 0, f)),
            pl.BlockSpec((None, width, tile), lambda f: (local, 0, f)),
            pl.BlockSpec((None, tile, width), lambda f: (local, f, 0)),
            pl.BlockSpec((n_out, n_rows), lambda f: (0, 0)),
        ],
        out_specs=pl.BlockSpec((n_out, width), lambda f: (0, 0)),
        out_shape=jax.ShapeDtypeStruct((n_out, width), jnp.bfloat16),
        scratch_shapes=[pltpu.VMEM((n_rows, width), jnp.float32)],
        compiler_params=pltpu.CompilerParams(vmem_limit_bytes=48 * 1024 * 1024),
    )(rows, w_gate, w_up, w_down, select)


def slot_match(expert_ids, experts, rows_here, n_groups):
    ids = expert_ids.reshape(n_groups, rows_here, expert_ids.shape[1])
    hit = jnp.any(ids[None, :, :, :] == experts[:, None, None, None], axis=-1)
    rank = jnp.cumsum(hit.astype(jnp.int32), axis=-1) - 1
    slot = jnp.arange(CAP, dtype=jnp.int32)
    return hit[:, :, None, :] & (rank[:, :, None, :] == slot[None, None, :, None])


def shards(
    query_rows, key_cache, value_cache, lengths, attn_gain, router, expert_ids, w_gate, w_up, w_down
):
    rows_here = query_rows.shape[0]
    span = key_cache.shape[1]
    kv_share = HEADS // KV_HEADS
    n_grp = lax.axis_size("grp")
    n_shard = lax.axis_size("shard")
    grp_id = lax.axis_index("grp")
    shard_id = lax.axis_index("shard")
    n_blocks = span // BLOCK

    query_heads = query_rows.reshape(rows_here, KV_HEADS, kv_share, HEAD_DIM)
    key_heads = key_cache.reshape(rows_here, span, KV_HEADS, HEAD_DIM)
    value_heads = value_cache.reshape(rows_here, n_blocks, BLOCK, KV_HEADS, HEAD_DIM)
    scores = jnp.einsum(
        "rgjd,rtgd->rgjt", query_heads, key_heads, preferred_element_type=jnp.float32
    ) / math.sqrt(HEAD_DIM)
    position = shard_id * span + jnp.arange(span, dtype=jnp.int32)
    live_mask = (position[None, :] < lengths[:, None])[:, None, None, :]
    scores = jnp.where(live_mask, scores, NEG_FILL)
    scores = scores.reshape(rows_here, KV_HEADS, kv_share, n_blocks, BLOCK)
    block_max = jnp.max(scores, axis=-1)
    block_probs = jnp.where(
        scores > 0.5 * NEG_FILL, jnp.exp(scores - block_max[..., None]), 0.0
    ).astype(jnp.bfloat16)
    block_sum = jnp.sum(block_probs.astype(jnp.float32), axis=-1)
    block_mix = jnp.einsum(
        "rgjbt,rbtgd->rgjbd", block_probs, value_heads, preferred_element_type=jnp.float32
    )
    dev_max = jnp.max(block_max, axis=-1)
    dev_factor = jnp.exp(block_max - dev_max[..., None])
    dev_sum = jnp.sum(block_sum * dev_factor, axis=-1).reshape(rows_here, HEADS)
    dev_mix = jnp.sum(block_mix * dev_factor[..., None], axis=-2).reshape(rows_here, HEADS, HEAD_DIM)
    dev_max = dev_max.reshape(rows_here, HEADS)

    per_chunk = HEADS // n_shard
    mix_out = dev_mix.reshape(rows_here, n_shard, per_chunk, HEAD_DIM)
    side = jnp.concatenate(
        [dev_max.reshape(rows_here, n_shard, per_chunk), dev_sum.reshape(rows_here, n_shard, per_chunk)],
        axis=-1,
    )
    side = jnp.pad(side, ((0, 0), (0, 0), (0, HEAD_DIM - 2 * per_chunk)))
    packed = jnp.concatenate([mix_out, side[:, :, None, :]], axis=2)
    packed = jnp.transpose(packed, (1, 0, 2, 3))
    stats = lax.all_to_all(packed, "shard", 0, 0, tiled=True)
    got_mix = stats[:, :, :per_chunk, :]
    got_max = stats[:, :, per_chunk, :per_chunk]
    got_sum = stats[:, :, per_chunk, per_chunk : 2 * per_chunk]
    top = jnp.max(got_max, axis=0)
    factor = jnp.exp(got_max - top[None])
    whole_sum = jnp.sum(got_sum * factor, axis=0)
    whole_mix = jnp.sum(got_mix * factor[..., None], axis=0)
    chunk = (whole_mix / whole_sum[..., None]).reshape(rows_here, per_chunk * HEAD_DIM)

    n_dev = n_grp * n_shard
    spread = jnp.broadcast_to(chunk.astype(jnp.bfloat16)[None], (n_dev,) + chunk.shape)
    gathered = lax.all_to_all(spread, ("grp", "shard"), 0, 0, tiled=True).astype(jnp.float32)
    gathered = gathered.reshape(n_grp, n_shard, rows_here, per_chunk * HEAD_DIM)
    attended = jnp.transpose(gathered, (0, 2, 1, 3)).reshape(n_grp * rows_here, -1)

    mean_square = jnp.mean(attended * attended, axis=-1, keepdims=True)
    normed_all = (attended * lax.rsqrt(mean_square + 1e-05) * attn_gain).astype(jnp.bfloat16)
    normed = lax.dynamic_slice_in_dim(normed_all, grp_id * rows_here, rows_here, 0)

    logits = jnp.dot(normed_all, router, preferred_element_type=jnp.float32)
    experts = router.shape[1]
    expert_range = jnp.arange(experts, dtype=jnp.int32)
    expert_hit = expert_ids[:, :, None] == expert_range[None, None, :]
    chosen = jnp.sum(jnp.where(expert_hit, logits[:, None, :], 0.0), axis=-1)
    first_weight = jax.nn.sigmoid(chosen[:, 0] - chosen[:, 1])
    route_weight = jnp.stack([first_weight, 1.0 - first_weight], axis=1)

    local_experts = w_gate.shape[0]
    assert local_experts == 1
    width = normed_all.shape[1]
    out_width = width // n_shard
    expert_index = grp_id
    coefficient = jnp.sum(jnp.where(expert_ids == expert_index, route_weight, 0.0), axis=-1)
    sending = slot_match(expert_ids, expert_index[None], rows_here, n_grp)[0]
    row_of = jnp.arange(n_grp * rows_here, dtype=jnp.int32).reshape(n_grp, 1, rows_here)
    select = jnp.sum(
        jnp.where(
            sending[..., None] & (row_of[..., None] == jnp.arange(n_grp * rows_here)[None, None, None, :]),
            coefficient[None, None, None, :],
            0.0,
        ),
        axis=2,
    )
    select = jnp.transpose(select, (1, 0, 2)).reshape(CAP * n_grp, n_grp * rows_here)
    picked = expert_ffn(normed_all, w_gate, w_up, w_down, 0, select)
    blocks = picked.reshape(CAP, n_dev, out_width)
    arrived = lax.all_to_all(blocks, ("grp", "shard"), 1, 1, tiled=True)
    arrived = arrived.astype(jnp.float32).reshape(CAP, n_grp, n_shard, out_width)
    per_expert = jnp.transpose(jnp.sum(arrived, axis=2), (1, 0, 2))
    own_ids = lax.dynamic_slice_in_dim(expert_ids, grp_id * rows_here, rows_here, 0)
    homes = slot_match(own_ids, jnp.arange(n_grp, dtype=jnp.int32) * local_experts, rows_here, 1)[:, 0]
    spread_back = jnp.where(homes[..., None], per_expert[:, :, None, :], 0.0)
    result = jnp.sum(spread_back, axis=(0, 1))
    return (normed, result.astype(jnp.bfloat16))


def solution(mesh):
    in_specs = (
        P("grp", None),
        P("grp", "shard", None),
        P("grp", "shard", None),
        P("grp"),
        P(),
        P(),
        P(),
        P("grp", None, "shard"),
        P("grp", None, "shard"),
        P("grp", "shard", None),
    )
    out_specs = (P("grp", None), P("grp", "shard"))
    return jax.shard_map(shards, mesh=mesh, in_specs=in_specs, out_specs=out_specs, check_vma=False)
```

```python
import math

import jax
import jax.numpy as jnp
from jax import lax
from jax.experimental import pallas as pl
from jax.experimental.pallas import tpu as pltpu
from jax.sharding import PartitionSpec as P

HEADS = 48
KV_HEADS = 8
HEAD_DIM = 128
BLOCK = 256


NEG_FILL = -1e30
CAP = 2


FF_TILE = 256


def expert_kernel(x_ref, gate_ref, up_ref, down_ref, sel_ref, out_ref, acc_ref):
    step = pl.program_id(0)

    @pl.when(step == 0)
    def _():
        acc_ref[...] = jnp.zeros_like(acc_ref)

    rows = x_ref[...]
    gate_proj = jnp.dot(rows, gate_ref[...], preferred_element_type=jnp.float32)
    up_proj = jnp.dot(rows, up_ref[...], preferred_element_type=jnp.float32)
    hidden = (jax.nn.silu(gate_proj) * up_proj).astype(jnp.bfloat16)
    acc_ref[...] += jnp.dot(hidden, down_ref[...], preferred_element_type=jnp.float32)

    @pl.when(step == pl.num_programs(0) - 1)
    def _():
        picked = jnp.dot(
            sel_ref[...], acc_ref[...], precision=lax.Precision.HIGHEST,
            preferred_element_type=jnp.float32,
        )
        out_ref[...] = picked.astype(out_ref.dtype)


def expert_ffn(rows, w_gate, w_up, w_down, local, select):
    n_rows, width = rows.shape
    n_out = select.shape[0]
    hidden_units = w_gate.shape[2]
    tile = min(FF_TILE, hidden_units)
    return pl.pallas_call(
        expert_kernel,
        grid=(hidden_units // tile,),
        in_specs=[
            pl.BlockSpec((n_rows, width), lambda f: (0, 0)),
            pl.BlockSpec((None, width, tile), lambda f: (local, 0, f)),
            pl.BlockSpec((None, width, tile), lambda f: (local, 0, f)),
            pl.BlockSpec((None, tile, width), lambda f: (local, f, 0)),
            pl.BlockSpec((n_out, n_rows), lambda f: (0, 0)),
        ],
        out_specs=pl.BlockSpec((n_out, width), lambda f: (0, 0)),
        out_shape=jax.ShapeDtypeStruct((n_out, width), jnp.bfloat16),
        scratch_shapes=[pltpu.VMEM((n_rows, width), jnp.float32)],
        compiler_params=pltpu.CompilerParams(vmem_limit_bytes=48 * 1024 * 1024),
    )(rows, w_gate, w_up, w_down, select)


def slot_match(expert_ids, experts, rows_here, n_groups):
    ids = expert_ids.reshape(n_groups, rows_here, expert_ids.shape[1])
    hit = jnp.any(ids[None, :, :, :] == experts[:, None, None, None], axis=-1)
    rank = jnp.cumsum(hit.astype(jnp.int32), axis=-1) - 1
    slot = jnp.arange(CAP, dtype=jnp.int32)
    return hit[:, :, None, :] & (rank[:, :, None, :] == slot[None, None, :, None])


def shards(
    query_rows, key_cache, value_cache, lengths, attn_gain, router, expert_ids, w_gate, w_up, w_down
):
    rows_here = query_rows.shape[0]
    span = key_cache.shape[1]
    kv_share = HEADS // KV_HEADS
    n_grp = lax.axis_size("grp")
    n_shard = lax.axis_size("shard")
    grp_id = lax.axis_index("grp")
    shard_id = lax.axis_index("shard")
    n_blocks = span // BLOCK

    query_heads = query_rows.reshape(rows_here, KV_HEADS, kv_share, HEAD_DIM)
    key_heads = key_cache.reshape(rows_here, span, KV_HEADS, HEAD_DIM)
    value_heads = value_cache.reshape(rows_here, n_blocks, BLOCK, KV_HEADS, HEAD_DIM)
    scores = jnp.einsum(
        "rgjd,rtgd->rgjt", query_heads, key_heads, preferred_element_type=jnp.float32
    ) / math.sqrt(HEAD_DIM)
    position = shard_id * span + jnp.arange(span, dtype=jnp.int32)
    live_mask = (position[None, :] < lengths[:, None])[:, None, None, :]
    scores = jnp.where(live_mask, scores, NEG_FILL)
    scores = scores.reshape(rows_here, KV_HEADS, kv_share, n_blocks, BLOCK)
    live_blocks = live_mask.reshape(rows_here, 1, 1, n_blocks, BLOCK)
    block_max = jnp.max(scores, axis=-1)
    block_probs = jnp.where(live_blocks, jnp.exp(scores - block_max[..., None]), 0.0).astype(
        jnp.bfloat16
    )
    block_sum = jnp.sum(block_probs.astype(jnp.float32), axis=-1)
    block_mix = jnp.einsum(
        "rgjbt,rbtgd->rgjbd", block_probs, value_heads, preferred_element_type=jnp.float32
    )
    if n_blocks == 1:
        dev_max = block_max[..., 0]
        dev_sum = block_sum[..., 0].reshape(rows_here, HEADS)
        dev_mix = block_mix[..., 0, :].reshape(rows_here, HEADS, HEAD_DIM)
    else:
        dev_max = jnp.max(block_max, axis=-1)
        dev_factor = jnp.exp(block_max - dev_max[..., None])
        dev_sum = jnp.sum(block_sum * dev_factor, axis=-1).reshape(rows_here, HEADS)
        dev_mix = jnp.sum(block_mix * dev_factor[..., None], axis=-2).reshape(rows_here, HEADS, HEAD_DIM)
    dev_max = dev_max.reshape(rows_here, HEADS)

    per_chunk = HEADS // n_shard
    mix_out = dev_mix.reshape(rows_here, n_shard, per_chunk, HEAD_DIM)
    side = jnp.concatenate(
        [dev_max.reshape(rows_here, n_shard, per_chunk), dev_sum.reshape(rows_here, n_shard, per_chunk)],
        axis=-1,
    )
    side = jnp.pad(side, ((0, 0), (0, 0), (0, HEAD_DIM - 2 * per_chunk)))
    packed = jnp.concatenate([mix_out, side[:, :, None, :]], axis=2)
    packed = jnp.transpose(packed, (1, 0, 2, 3))
    stats = lax.all_to_all(packed, "shard", 0, 0, tiled=True)
    got_mix = stats[:, :, :per_chunk, :]
    got_max = stats[:, :, per_chunk, :per_chunk]
    got_sum = stats[:, :, per_chunk, per_chunk : 2 * per_chunk]
    top = jnp.max(got_max, axis=0)
    factor = jnp.exp(got_max - top[None])
    whole_sum = jnp.sum(got_sum * factor, axis=0)
    whole_mix = jnp.sum(got_mix * factor[..., None], axis=0)
    chunk = (whole_mix / whole_sum[..., None]).reshape(rows_here, per_chunk * HEAD_DIM)

    n_dev = n_grp * n_shard
    spread = jnp.broadcast_to(chunk.astype(jnp.bfloat16)[None], (n_dev,) + chunk.shape)
    gathered = lax.all_to_all(spread, ("grp", "shard"), 0, 0, tiled=True).astype(jnp.float32)
    gathered = gathered.reshape(n_grp, n_shard, rows_here, per_chunk * HEAD_DIM)
    attended = jnp.transpose(gathered, (0, 2, 1, 3)).reshape(n_grp * rows_here, -1)

    mean_square = jnp.mean(attended * attended, axis=-1, keepdims=True)
    normed_all = (attended * lax.rsqrt(mean_square + 1e-05) * attn_gain).astype(jnp.bfloat16)
    normed = lax.dynamic_slice_in_dim(normed_all, grp_id * rows_here, rows_here, 0)

    logits = jnp.dot(normed_all, router, preferred_element_type=jnp.float32)
    experts = router.shape[1]
    expert_range = jnp.arange(experts, dtype=jnp.int32)
    expert_hit = expert_ids[:, :, None] == expert_range[None, None, :]
    chosen = jnp.sum(jnp.where(expert_hit, logits[:, None, :], 0.0), axis=-1)
    first_weight = jax.nn.sigmoid(chosen[:, 0] - chosen[:, 1])
    route_weight = jnp.stack([first_weight, 1.0 - first_weight], axis=1)

    local_experts = w_gate.shape[0]
    assert local_experts == 1
    width = normed_all.shape[1]
    out_width = width // n_shard
    expert_index = grp_id
    coefficient = jnp.sum(jnp.where(expert_ids == expert_index, route_weight, 0.0), axis=-1)
    sending = slot_match(expert_ids, expert_index[None], rows_here, n_grp)[0]
    row_of = jnp.arange(n_grp * rows_here, dtype=jnp.int32).reshape(n_grp, 1, rows_here)
    select = jnp.sum(
        jnp.where(
            sending[..., None] & (row_of[..., None] == jnp.arange(n_grp * rows_here)[None, None, None, :]),
            coefficient[None, None, None, :],
            0.0,
        ),
        axis=2,
    )
    select = jnp.transpose(select, (1, 0, 2)).reshape(CAP * n_grp, n_grp * rows_here)
    picked = expert_ffn(normed_all, w_gate, w_up, w_down, 0, select)
    blocks = picked.reshape(CAP, n_dev, out_width)
    arrived = lax.all_to_all(blocks, ("grp", "shard"), 1, 1, tiled=True)
    arrived = arrived.astype(jnp.float32).reshape(CAP, n_grp, n_shard, out_width)
    per_expert = jnp.transpose(jnp.sum(arrived, axis=2), (1, 0, 2))
    own_ids = lax.dynamic_slice_in_dim(expert_ids, grp_id * rows_here, rows_here, 0)
    homes = slot_match(own_ids, jnp.arange(n_grp, dtype=jnp.int32) * local_experts, rows_here, 1)[:, 0]
    spread_back = jnp.where(homes[..., None], per_expert[:, :, None, :], 0.0)
    result = jnp.sum(spread_back, axis=(0, 1))
    return (normed, result.astype(jnp.bfloat16))


def solution(mesh):
    in_specs = (
        P("grp", None),
        P("grp", "shard", None),
        P("grp", "shard", None),
        P("grp"),
        P(),
        P(),
        P(),
        P("grp", None, "shard"),
        P("grp", None, "shard"),
        P("grp", "shard", None),
    )
    out_specs = (P("grp", None), P("grp", "shard"))
    return jax.shard_map(shards, mesh=mesh, in_specs=in_specs, out_specs=out_specs, check_vma=False)
```

```python
import math

import jax
import jax.numpy as jnp
from jax import lax
from jax.experimental import pallas as pl
from jax.experimental.pallas import tpu as pltpu
from jax.sharding import PartitionSpec as P

HEADS = 48
KV_HEADS = 8
HEAD_DIM = 128
BLOCK = 256


NEG_FILL = -1e30
CAP = 2


FF_TILE = 256


def expert_kernel(x_ref, gate_ref, up_ref, down_ref, sel_ref, out_ref, acc_ref):
    step = pl.program_id(0)

    @pl.when(step == 0)
    def _():
        acc_ref[...] = jnp.zeros_like(acc_ref)

    rows = x_ref[...]
    gate_proj = jnp.dot(rows, gate_ref[...], preferred_element_type=jnp.float32)
    up_proj = jnp.dot(rows, up_ref[...], preferred_element_type=jnp.float32)
    hidden = (jax.nn.silu(gate_proj) * up_proj).astype(jnp.bfloat16)
    acc_ref[...] += jnp.dot(hidden, down_ref[...], preferred_element_type=jnp.float32)

    @pl.when(step == pl.num_programs(0) - 1)
    def _():
        picked = jnp.dot(
            sel_ref[...], acc_ref[...], precision=lax.Precision.HIGHEST,
            preferred_element_type=jnp.float32,
        )
        out_ref[...] = picked.astype(out_ref.dtype)


def expert_ffn(rows, w_gate, w_up, w_down, local, select):
    n_rows, width = rows.shape
    n_out = select.shape[0]
    hidden_units = w_gate.shape[2]
    tile = min(FF_TILE, hidden_units)
    return pl.pallas_call(
        expert_kernel,
        grid=(hidden_units // tile,),
        in_specs=[
            pl.BlockSpec((n_rows, width), lambda f: (0, 0)),
            pl.BlockSpec((None, width, tile), lambda f: (local, 0, f)),
            pl.BlockSpec((None, width, tile), lambda f: (local, 0, f)),
            pl.BlockSpec((None, tile, width), lambda f: (local, f, 0)),
            pl.BlockSpec((n_out, n_rows), lambda f: (0, 0)),
        ],
        out_specs=pl.BlockSpec((n_out, width), lambda f: (0, 0)),
        out_shape=jax.ShapeDtypeStruct((n_out, width), jnp.bfloat16),
        scratch_shapes=[pltpu.VMEM((n_rows, width), jnp.float32)],
        compiler_params=pltpu.CompilerParams(vmem_limit_bytes=48 * 1024 * 1024),
    )(rows, w_gate, w_up, w_down, select)


def slot_match(expert_ids, experts, rows_here, n_groups):
    ids = expert_ids.reshape(n_groups, rows_here, expert_ids.shape[1])
    hit = jnp.any(ids[None, :, :, :] == experts[:, None, None, None], axis=-1)
    rank = jnp.cumsum(hit.astype(jnp.int32), axis=-1) - 1
    slot = jnp.arange(CAP, dtype=jnp.int32)
    return hit[:, :, None, :] & (rank[:, :, None, :] == slot[None, None, :, None])


def shards(
    query_rows, key_cache, value_cache, lengths, attn_gain, router, expert_ids, w_gate, w_up, w_down
):
    rows_here = query_rows.shape[0]
    span = key_cache.shape[1]
    kv_share = HEADS // KV_HEADS
    n_grp = lax.axis_size("grp")
    n_shard = lax.axis_size("shard")
    grp_id = lax.axis_index("grp")
    shard_id = lax.axis_index("shard")
    n_blocks = span // BLOCK

    query_heads = query_rows.reshape(rows_here, KV_HEADS, kv_share, HEAD_DIM)
    key_heads = key_cache.reshape(rows_here, span, KV_HEADS, HEAD_DIM)
    value_heads = value_cache.reshape(rows_here, n_blocks, BLOCK, KV_HEADS, HEAD_DIM)
    scores = jnp.einsum(
        "rgjd,rtgd->rgjt", query_heads, key_heads, preferred_element_type=jnp.float32
    ) / math.sqrt(HEAD_DIM)
    position = shard_id * span + jnp.arange(span, dtype=jnp.int32)
    live_mask = (position[None, :] < lengths[:, None])[:, None, None, :]
    scores = jnp.where(live_mask, scores, NEG_FILL)
    scores = scores.reshape(rows_here, KV_HEADS, kv_share, n_blocks, BLOCK)
    live_blocks = live_mask.reshape(rows_here, 1, 1, n_blocks, BLOCK)
    block_max = jnp.max(scores, axis=-1)
    block_probs = jnp.where(live_blocks, jnp.exp(scores - block_max[..., None]), 0.0).astype(
        jnp.bfloat16
    )
    block_sum = jnp.sum(block_probs.astype(jnp.float32), axis=-1)
    block_mix = jnp.einsum(
        "rgjbt,rbtgd->rgjbd", block_probs, value_heads, preferred_element_type=jnp.float32
    )
    dev_max = jnp.max(block_max, axis=-1)
    dev_factor = jnp.exp(block_max - dev_max[..., None])
    dev_sum = jnp.sum(block_sum * dev_factor, axis=-1).reshape(rows_here, HEADS)
    dev_mix = jnp.sum(block_mix * dev_factor[..., None], axis=-2).reshape(rows_here, HEADS, HEAD_DIM)
    dev_max = dev_max.reshape(rows_here, HEADS)

    per_chunk = HEADS // n_shard
    mix_out = dev_mix.reshape(rows_here, n_shard, per_chunk, HEAD_DIM)
    side = jnp.concatenate(
        [dev_max.reshape(rows_here, n_shard, per_chunk), dev_sum.reshape(rows_here, n_shard, per_chunk)],
        axis=-1,
    )
    side = jnp.pad(side, ((0, 0), (0, 0), (0, HEAD_DIM - 2 * per_chunk)))
    packed = jnp.concatenate([mix_out, side[:, :, None, :]], axis=2)
    packed = jnp.transpose(packed, (1, 0, 2, 3))
    stats = lax.all_to_all(packed, "shard", 0, 0, tiled=True)
    got_mix = stats[:, :, :per_chunk, :]
    got_max = stats[:, :, per_chunk, :per_chunk]
    got_sum = stats[:, :, per_chunk, per_chunk : 2 * per_chunk]
    top = jnp.max(got_max, axis=0)
    factor = jnp.exp(got_max - top[None])
    whole_sum = jnp.sum(got_sum * factor, axis=0)
    whole_mix = jnp.sum(got_mix * factor[..., None], axis=0)
    chunk = (whole_mix / whole_sum[..., None]).reshape(rows_here, per_chunk * HEAD_DIM)

    n_dev = n_grp * n_shard
    spread = jnp.broadcast_to(chunk.astype(jnp.bfloat16)[None], (n_dev,) + chunk.shape)
    gathered = lax.all_to_all(spread, ("grp", "shard"), 0, 0, tiled=True).astype(jnp.float32)
    gathered = gathered.reshape(n_grp, n_shard, rows_here, per_chunk * HEAD_DIM)
    attended = jnp.transpose(gathered, (0, 2, 1, 3)).reshape(n_grp * rows_here, -1)

    mean_square = jnp.mean(attended * attended, axis=-1, keepdims=True)
    normed_all = (attended * lax.rsqrt(mean_square + 1e-05) * attn_gain).astype(jnp.bfloat16)
    normed = lax.dynamic_slice_in_dim(normed_all, grp_id * rows_here, rows_here, 0)

    logits = jnp.dot(normed_all, router, preferred_element_type=jnp.float32)
    experts = router.shape[1]
    expert_range = jnp.arange(experts, dtype=jnp.int32)
    expert_hit = expert_ids[:, :, None] == expert_range[None, None, :]
    chosen = jnp.sum(jnp.where(expert_hit, logits[:, None, :], 0.0), axis=-1)
    first_weight = jax.nn.sigmoid(chosen[:, 0] - chosen[:, 1])
    route_weight = jnp.stack([first_weight, 1.0 - first_weight], axis=1)

    local_experts = w_gate.shape[0]
    assert local_experts == 1
    width = normed_all.shape[1]
    out_width = width // n_shard
    expert_index = grp_id
    sending = slot_match(expert_ids, expert_index[None], rows_here, n_grp)[0]
    row_of = jnp.arange(n_grp * rows_here, dtype=jnp.int32).reshape(n_grp, 1, rows_here)
    select = jnp.sum(
        jnp.where(
            sending[..., None] & (row_of[..., None] == jnp.arange(n_grp * rows_here)[None, None, None, :]),
            1.0,
            0.0,
        ),
        axis=2,
    )
    select = jnp.transpose(select, (1, 0, 2)).reshape(CAP * n_grp, n_grp * rows_here)
    picked = expert_ffn(normed_all, w_gate, w_up, w_down, 0, select)
    blocks = picked.reshape(CAP, n_dev, out_width)
    arrived = lax.all_to_all(blocks, ("grp", "shard"), 1, 1, tiled=True)
    arrived = arrived.astype(jnp.float32).reshape(CAP, n_grp, n_shard, out_width)
    per_expert = jnp.transpose(jnp.sum(arrived, axis=2), (1, 0, 2))
    own_ids = lax.dynamic_slice_in_dim(expert_ids, grp_id * rows_here, rows_here, 0)
    homes = slot_match(own_ids, jnp.arange(n_grp, dtype=jnp.int32) * local_experts, rows_here, 1)[:, 0]
    own_weight = lax.dynamic_slice_in_dim(route_weight, grp_id * rows_here, rows_here, 0)
    expert_weight = jnp.sum(
        jnp.where(
            own_ids[None, :, :] == (jnp.arange(n_grp, dtype=jnp.int32) * local_experts)[:, None, None],
            own_weight[None, :, :],
            0.0,
        ),
        axis=-1,
    )
    spread_back = jnp.where(
        homes[..., None], per_expert[:, :, None, :] * expert_weight[:, None, :, None], 0.0
    )
    result = jnp.sum(spread_back, axis=(0, 1))
    return (normed, result.astype(jnp.bfloat16))


def solution(mesh):
    in_specs = (
        P("grp", None),
        P("grp", "shard", None),
        P("grp", "shard", None),
        P("grp"),
        P(),
        P(),
        P(),
        P("grp", None, "shard"),
        P("grp", None, "shard"),
        P("grp", "shard", None),
    )
    out_specs = (P("grp", None), P("grp", "shard"))
    return jax.shard_map(shards, mesh=mesh, in_specs=in_specs, out_specs=out_specs, check_vma=False)
```
